256 devices in a mesh: req: 2 (over core), seq: 16 (over y, x), tp: 8 (over z).
Axes of the slice: x: 4, y: 4, z: 8, core: 2. Of those that a mesh axis runs over, the one named last changes fastest.
Arguments:
- queries: bfloat16 [4, 512, 3072], P('req', 'seq', 'tp'), may hold values from -48 to 48
- new_kv: bfloat16 [4, 512, 2, 3072], P('req', 'seq', None, 'tp'), may hold values from -4 to 4
- cache_kv: bfloat16 [4, 16384, 2, 3072], P('req', 'seq', None, 'tp'), may hold values from -4 to 4
- cached_len: int32 [4], P('req'), may hold values from 1 to 16384, as said below
- residual_in: bfloat16 [4, 512, 3072], P('req', 'seq', 'tp'), may hold values from -1.5 to 1.5
- norm_gain: float32 [3072], replicated, may hold values from 0.1 to 1.9
- gate_w: bfloat16 [3072, 4096], P(None, 'tp'), may hold values from -0.109375 to 0.109375
- up_w: bfloat16 [3072, 4096], P(None, 'tp'), may hold values from -0.109375 to 0.109375
- down_w: bfloat16 [4096, 3072], P('tp'), may hold values from -0.09375 to 0.09375
- owner: int32 [32, 64, 1], P(('req', 'seq')), may hold values from 0 to 31; in each aligned block of 64 rows (0 to 63, 64 to 127, ..., all dimensions but the last counted through in order) at most 4 rows name the same one
Outputs:
- layer_out: bfloat16 [32, 32, 4, 3072], P(('req', 'seq'), None, None, 'tp')
The draws below stay inside these ranges and needn't reach their ends.
Inputs may be any that keep to these rules, and one draw needn't show every extreme that they name: `cached_len`: exactly 1 request have 16384 - 16384 // 8 cached positions or more, one of them exactly 16384; every other request has at most 1024. Within one row block no owner is named by more than 4 rows.
All inputs are finite; a program needn't handle non-finite values.
Results may differ from the reference program's by a relative error of at most 0.02.
Values may be sent and summed in bfloat16 or wider, within the bound.
No kernel may reach another device: no remote copies, remote signals or barrier semaphores. Data moves between devices by JAX's collectives and lax.ppermute only.
A program may use at most 256 MiB of HBM per device.

```python
import math
import jax
import jax.numpy as jnp
import numpy as np
from jax import lax

HEADS = 32
HEAD = 96
WIDTH = 3072
UNITS = 4096
NEW = 512
CAP = 16384
SLOTS = 2
REQUESTS = 4
TOKS = 32
ROWS = 64
OWNERS = 32
SLOTCAP = 4
SHORT = 1024
LONGS = 1
N_REQ = 2
N_SEQ = 16


def attention_draw(key):
    key_query, key_fresh, key_cached, key_anchor, key_size, key_sign, key_heavy = jax.random.split(jax.random.fold_in(key, 7), 7)
    fresh_shape = (REQUESTS, NEW, 2, WIDTH)
    cached_shape = (REQUESTS, CAP, 2, WIDTH)
    queries = jnp.clip(2.0 * jax.random.normal(key_query, (REQUESTS, NEW, WIDTH), jnp.float32), -12.0, 12.0)
    fresh = jnp.clip(jax.random.normal(key_fresh, fresh_shape, jnp.float32), -4.0, 4.0)
    cached = jnp.clip(jax.random.normal(key_cached, cached_shape, jnp.float32), -4.0, 4.0)
    middle = NEW // 2
    quarter = NEW // 4
    anchors = jax.random.uniform(key_anchor, (3, REQUESTS, WIDTH), jnp.float32, -2.0, 2.0)
    for section_index, strength in enumerate((60.0, 110.0, 170.0)):
        anchor = anchors[section_index]
        factor = 0.75 * strength / math.sqrt(HEAD)
        first_pos = quarter + section_index
        fresh = fresh.at[:, first_pos, 0, :].set(anchor)
        fresh = fresh.at[:, first_pos + TOKS, 0, :].set(anchor * (1.0 - 2.0 / strength))
        queries = queries.at[:, NEW - 1 - section_index, :].set(factor * anchor)
    magnitude = jax.random.uniform(key_size, (REQUESTS, WIDTH), jnp.float32, 0.5, 1.0)
    strong_sign = jnp.where(jax.random.bernoulli(key_sign, 0.5, (REQUESTS, WIDTH)), 4.0, -4.0)
    strong = magnitude * strong_sign
    top_strength = 420.0
    top_factor = top_strength * 12.0 / (112.0 * math.sqrt(HEAD))
    top_pos = quarter + 3
    fresh = fresh.at[:, top_pos + TOKS, 0, :].set(strong)
    fresh = fresh.at[:, top_pos, 0, :].set(strong * (1.0 - 2.0 / top_strength))
    queries = queries.at[:, NEW - 4, :].set(top_factor * strong)
    heavy = jnp.where(jax.random.bernoulli(key_heavy, 0.5, (REQUESTS, WIDTH)), 4.0, -4.0)
    fresh = fresh.at[:, middle + 8, 0, :].set(heavy)
    return (queries, fresh, cached)


def draw_queries(key, part):
    return attention_draw(key)[0].astype(jnp.bfloat16)


def draw_new_kv(key, part):
    return attention_draw(key)[1].astype(jnp.bfloat16)


def draw_cache_kv(key, part):
    return attention_draw(key)[2].astype(jnp.bfloat16)


def draw_cached_len(key, part):
    key_order, key_short, key_long = jax.random.split(jax.random.fold_in(key, 29), 3)
    ordering = jax.random.permutation(key_order, REQUESTS).astype(jnp.int32)
    ranking = jnp.zeros((REQUESTS,), jnp.int32).at[ordering].set(jnp.arange(REQUESTS, dtype=jnp.int32))
    shorter = jax.random.randint(key_short, (REQUESTS,), 1, SHORT + 1)
    longer = jax.random.randint(key_long, (REQUESTS,), CAP - CAP // 8, CAP + 1)
    return jnp.where(ranking == 0, CAP, jnp.where(ranking < LONGS, longer, shorter)).astype(jnp.int32)


def block_scale(stream_key, extent, cuts, smallest, high):
    level = 1.0
    for dim, blocks in cuts:
        steps = jax.random.uniform(jax.random.fold_in(jax.random.fold_in(stream_key, 6), dim), (blocks,), jnp.float32, smallest / len(cuts), high / len(cuts))
        level = level * jnp.repeat(jnp.exp(steps), extent[dim] // blocks).reshape((-1,) + (1,) * (len(extent) - 1 - dim))
    return level


def deal_out(rng, own, number, rows, number_of, top, reach, skew):
    sequence = jax.random.permutation(rng, number_of)
    packed, usual = load_shares(number_of, rows * top, reach, skew, True), load_shares(number_of, rows * top, reach, skew, False)
    places = jnp.arange(number_of)

    def named(sizes, turn):
        used = int((sizes > 0).sum())
        fixed = max(1, used // 4)
        passed = fixed + (places - fixed + turn * (used - fixed)) % max(1, number_of - fixed)
        return jnp.zeros((number_of,), jnp.int32).at[sequence[jnp.where(places < fixed, places, passed)]].set(jnp.asarray(sizes, jnp.int32))

    sizes = jnp.where(number % 4 == 0, named(packed, number // 4), named(usual, number - number // 4 - 1))
    mixed = jax.random.permutation(jax.random.fold_in(own, 3), number_of)
    giver, receiver = mixed[0:number_of // 2 * 2:2], mixed[1:number_of // 2 * 2:2]
    margin = jnp.minimum(sizes[giver] - 1, reach - sizes[receiver]) // 2
    margin = jnp.where((giver == sequence[0]) | (receiver == sequence[0]) | (sizes[receiver] == 0), 0, jnp.maximum(margin, 0))
    passed = jax.random.randint(jax.random.fold_in(own, 4), (number_of // 2,), 0, 1 << 20) % (margin + 1)
    sizes = sizes.at[giver].add(-passed).at[receiver].add(passed)
    members = jnp.searchsorted(jnp.cumsum(sizes), jnp.arange(rows * top), side="right").astype(jnp.int32)
    listing = members.reshape(top, rows).T
    listing = listing[jax.random.permutation(jax.random.fold_in(own, 1), rows)]
    turn = jax.random.randint(jax.random.fold_in(own, 2), (rows, 1), 0, top)
    return jnp.take_along_axis(listing, (jnp.arange(top)[None, :] + turn) % top, axis=1)


def load_shares(count, total, most, slope, full):
    loads = [(1 << 20) // math.isqrt(grade ** slope) + 1 for grade in range(1, count + 1)]
    largest = most if full else min(most, max(-(-total // count), total * loads[0] // sum(loads)))
    least = 1 if total - largest >= count - 1 else 0
    given, surplus = [largest] + [least] * (count - 1), total - largest - least * (count - 1)
    while surplus > 0:
        candidates = [i for i in range(1, count) if given[i] < largest] or [i for i in range(1, count) if given[i] < most]
        mass, left = sum([loads[i] for i in candidates]), surplus
        for i in candidates:
            more = min(most - given[i], max(1, left * loads[i] // mass), surplus)
            given[i] = given[i] + more
            surplus = surplus - more
    return np.array(given)


def bell_draw(rng, dims, deviation, reach, shards=(), held_as=jnp.bfloat16):
    array = deviation * jax.random.normal(rng, dims, jnp.float32)
    if shards:
        array = array * block_scale(rng, dims, shards, -0.22, 0.18)
    return jnp.clip(array, -reach, reach).astype(held_as)


def setup_inputs(seed: int = 0) -> dict:
    seeds = jax.random.split(jax.random.key(seed), 11)
    queries = draw_queries(jax.random.fold_in(seeds[10], 71), 0)
    new_kv = draw_new_kv(jax.random.fold_in(seeds[10], 71), 0)
    cache_kv = draw_cache_kv(jax.random.fold_in(seeds[10], 71), 0)
    cached_len = draw_cached_len(jax.random.fold_in(seeds[10], 71), 0)
    residual_in = bell_draw(seeds[4], (REQUESTS, NEW, WIDTH), 0.25, 1.5, ((0, 2), (1, 16), (2, 8)))
    norm_gain = jnp.clip(1.0 + 0.18 * jax.random.normal(seeds[5], (WIDTH,), jnp.float32), 0.1, 1.9)
    gate_w = bell_draw(seeds[6], (WIDTH, UNITS), WIDTH ** -0.5, 0.109375, ((1, 8),))
    up_w = bell_draw(seeds[7], (WIDTH, UNITS), WIDTH ** -0.5, 0.109375, ((1, 8),))
    down_w = bell_draw(seeds[8], (UNITS, WIDTH), UNITS ** -0.5, 0.09375, ((0, 8),))
    owner_keys = jax.random.split(jax.random.fold_in(seeds[9], 1), OWNERS * ROWS // ROWS)
    owner_turns = jax.random.permutation(jax.random.fold_in(seeds[9], 3), OWNERS * ROWS // ROWS)
    owner = jax.vmap(lambda own, number: deal_out(jax.random.fold_in(seeds[9], 2), own, number, ROWS, OWNERS, 1, SLOTCAP, 2))(owner_keys, owner_turns).reshape((OWNERS, ROWS, 1))
    return {"queries": queries, "new_kv": new_kv, "cache_kv": cache_kv, "cached_len": cached_len, "residual_in": residual_in, "norm_gain": norm_gain, "gate_w": gate_w, "up_w": up_w, "down_w": down_w, "owner": owner}


def one_head(operands):
    query_head, key_head, value_head, visible = operands
    scores = jnp.einsum('qd,kd->qk', query_head.astype(jnp.float32), key_head.astype(jnp.float32)) * HEAD ** (-0.5)
    masked = jnp.where(visible, scores, -1e+30)
    row_peak = lax.optimization_barrier(jnp.max(masked, axis=-1, keepdims=True))
    weights = jnp.where(visible, jnp.exp(masked - row_peak), 0.0)
    row_total = lax.optimization_barrier(jnp.sum(weights, axis=-1))
    rounded = lax.optimization_barrier(weights.astype(jnp.bfloat16))
    weighted = jnp.einsum('qk,kd->qd', rounded.astype(jnp.float32), value_head.astype(jnp.float32))
    return weighted / row_total[:, None]

def attend(operands):
    query_block, fresh_block, cached_block, length = operands
    keys_all = jnp.concatenate([cached_block[:, 0], fresh_block[:, 0]], axis=0).reshape(CAP + NEW, HEADS, HEAD).transpose(1, 0, 2)
    values_all = jnp.concatenate([cached_block[:, 1], fresh_block[:, 1]], axis=0).reshape(CAP + NEW, HEADS, HEAD).transpose(1, 0, 2)
    query_heads = query_block.reshape(NEW, HEADS, HEAD).transpose(1, 0, 2)
    positions = jnp.arange(NEW, dtype=jnp.int32)
    cached_visible = jnp.broadcast_to((jnp.arange(CAP, dtype=jnp.int32) < length)[None, :], (NEW, CAP))
    fresh_visible = positions[None, :] <= positions[:, None]
    visible = jnp.concatenate([cached_visible, fresh_visible], axis=1)
    visible_all = jnp.broadcast_to(visible[None], (HEADS, NEW, CAP + NEW))
    result = lax.map(one_head, (query_heads, keys_all, values_all, visible_all))
    return result.transpose(1, 0, 2).reshape(NEW, WIDTH)

def reference(queries, new_kv, cache_kv, cached_len, residual_in, norm_gain, gate_w, up_w, down_w, owner):
    attention = lax.map(attend, (queries, new_kv, cache_kv, cached_len))
    stream = (residual_in.astype(jnp.float32) + attention).astype(jnp.bfloat16)
    blocks = stream.reshape(N_REQ, SLOTS, N_SEQ, TOKS, WIDTH).transpose(0, 2, 1, 3, 4).reshape(OWNERS, ROWS, WIDTH)

    def feed_forward(block_rows):
        values = block_rows.astype(jnp.float32)
        mean_square = lax.optimization_barrier(jnp.mean(values * values, axis=-1, keepdims=True))
        normed = (values * lax.rsqrt(mean_square + 1e-05) * norm_gain).astype(jnp.bfloat16)
        gate_out = jnp.dot(normed, gate_w, preferred_element_type=jnp.float32)
        up_out = jnp.dot(normed, up_w, preferred_element_type=jnp.float32)
        hidden = (jax.nn.silu(gate_out) * up_out).astype(jnp.bfloat16)
        return (values + jnp.dot(hidden, down_w, preferred_element_type=jnp.float32)).astype(jnp.bfloat16)
    finished = lax.map(feed_forward, blocks)
    owner_ids = owner[:, :, 0].astype(jnp.int32)
    matches = (owner_ids[:, :, None] == jnp.arange(OWNERS, dtype=jnp.int32)[None, None, :]).astype(jnp.int32)
    ranking = lax.optimization_barrier(jnp.sum(jnp.cumsum(matches, axis=1) * matches, axis=2)) - 1
    block_ids = jnp.broadcast_to(jnp.arange(OWNERS, dtype=jnp.int32)[:, None], (OWNERS, ROWS))
    layer_out = jnp.zeros((OWNERS, OWNERS, SLOTCAP, WIDTH), jnp.bfloat16)
    return layer_out.at[owner_ids, block_ids, ranking].set(finished)
```

```python
import functools

import jax
import jax.numpy as jnp
from jax import lax
from jax.experimental import pallas as pl
from jax.experimental.pallas import tpu as pltpu
from jax.sharding import PartitionSpec as P

HEAD = 96

masked_floor = -1e30

STAT_LANES = 128
TOTAL_LANE = 8


def attention_kernel(meta_ref, q_ref, kc_ref, vc_ref, kf_ref, vf_ref, out_ref, *, tq, heads):
    slot = pl.program_id(0)
    q_block = pl.program_id(1)
    seq_index = meta_ref[0]
    length = meta_ref[1 + slot]
    span = kc_ref.shape[0]
    fresh_count = kf_ref.shape[0]
    width = q_ref.shape[1]
    offset = seq_index * span
    scale = HEAD ** (-0.5)

    q = q_ref[...]
    lane = lax.broadcasted_iota(jnp.int32, (1, width), 1)
    stat_lane = lax.broadcasted_iota(jnp.int32, (1, STAT_LANES), 1)
    rows = q_block * tq + lax.broadcasted_iota(jnp.int32, (tq, 1), 0)
    fresh_cols = seq_index * fresh_count + lax.broadcasted_iota(jnp.int32, (1, fresh_count), 1)
    fresh_visible = fresh_cols <= rows
    cached_visible = (offset + lax.broadcasted_iota(jnp.int32, (1, span), 1)) < length
    contract = (((1,), (1,)), ((), ()))

    def run(with_cache):
        kf = kf_ref[...]
        vf = vf_ref[...]
        if with_cache:
            kc = kc_ref[...]
            vc = vc_ref[...]
        weighted = jnp.zeros((tq, width), jnp.float32)
        stats = jnp.zeros((tq, STAT_LANES), jnp.float32)
        for h in range(heads):
            head_lanes = (lane >= h * HEAD) & (lane < (h + 1) * HEAD)
            qh = jnp.where(head_lanes, q, jnp.zeros_like(q))
            sf = lax.dot_general(qh, kf, contract, preferred_element_type=jnp.float32) * scale
            sf = jnp.where(fresh_visible, sf, masked_floor)
            peak = jnp.max(sf, axis=-1, keepdims=True)
            if with_cache:
                sc = lax.dot_general(qh, kc, contract, preferred_element_type=jnp.float32) * scale
                sc = jnp.where(cached_visible, sc, masked_floor)
                peak = jnp.maximum(peak, jnp.max(sc, axis=-1, keepdims=True))
            pf = jnp.where(fresh_visible, jnp.exp(sf - peak), 0.0)
            total = jnp.sum(pf, axis=-1, keepdims=True)
            oh = jnp.dot(pf.astype(jnp.bfloat16), vf, preferred_element_type=jnp.float32)
            if with_cache:
                pc = jnp.where(cached_visible, jnp.exp(sc - peak), 0.0)
                total = total + jnp.sum(pc, axis=-1, keepdims=True)
                oh = oh + jnp.dot(pc.astype(jnp.bfloat16), vc, preferred_element_type=jnp.float32)
            weighted = jnp.where(head_lanes, oh, weighted)
            stats = jnp.where(stat_lane == h, peak, stats)
            stats = jnp.where(stat_lane == TOTAL_LANE + h, total, stats)
        out_ref[:, :width] = weighted
        out_ref[:, width:] = stats

    @pl.when(offset < length)
    def _():
        run(True)

    @pl.when(offset >= length)
    def _():
        run(False)


def local_attention(all_queries, cache_kv, new_kv, cached_len, seq_index):
    slot_count, query_count, width = all_queries.shape
    span = cache_kv.shape[1]
    fresh_count = new_kv.shape[1]
    heads = width // HEAD
    tq = 256 if query_count % 256 == 0 else query_count
    cache2 = cache_kv.reshape(slot_count, span, 2 * width)
    fresh2 = new_kv.reshape(slot_count, fresh_count, 2 * width)
    meta = jnp.concatenate([jnp.reshape(seq_index, (1,)).astype(jnp.int32), cached_len.astype(jnp.int32)])
    kernel = functools.partial(attention_kernel, tq=tq, heads=heads)
    grid_spec = pltpu.PrefetchScalarGridSpec(
        num_scalar_prefetch=1,
        grid=(slot_count, query_count // tq),
        in_specs=[
            pl.BlockSpec((None, tq, width), lambda s, b, m: (s, b, 0)),
            pl.BlockSpec((None, span, width), lambda s, b, m: (s, 0, 0)),
            pl.BlockSpec((None, span, width), lambda s, b, m: (s, 0, 1)),
            pl.BlockSpec((None, fresh_count, width), lambda s, b, m: (s, 0, 0)),
            pl.BlockSpec((None, fresh_count, width), lambda s, b, m: (s, 0, 1)),
        ],
        out_specs=pl.BlockSpec((None, tq, width + STAT_LANES), lambda s, b, m: (s, b, 0)),
    )
    return pl.pallas_call(
        kernel,
        grid_spec=grid_spec,
        out_shape=jax.ShapeDtypeStruct((slot_count, query_count, width + STAT_LANES), jnp.float32),
    )(meta, all_queries, cache2, cache2, fresh2, fresh2)


def normalize(features, norm_gain):
    values = features.astype(jnp.float32)
    mean_square = jnp.mean(values * values, axis=-1, keepdims=True)
    return (values * lax.rsqrt(mean_square + 1e-05) * norm_gain).astype(jnp.bfloat16)


def per_device(
    queries, new_kv, cache_kv, cached_len, residual_in, norm_gain, gate_w, up_w, down_w, owner
):
    slot_count, token_count, width_local = queries.shape
    head_count = width_local // HEAD
    seq_index = lax.axis_index("seq")
    all_queries = lax.all_gather(queries, "seq", axis=1, tiled=True)
    packed = local_attention(all_queries, cache_kv, new_kv, cached_len, seq_index)
    source = lax.all_to_all(packed[None], "seq", split_axis=2, concat_axis=0, tiled=True)
    source_sum = source[..., :width_local]
    source_peak = source[..., width_local:width_local + head_count]
    source_total = source[..., width_local + TOTAL_LANE:width_local + TOTAL_LANE + head_count]
    joint_peak = jnp.max(source_peak, axis=0)
    source_scale = jnp.exp(source_peak - joint_peak[None])
    own_total = jnp.sum(source_total * source_scale, axis=0)
    grouped = source_sum.reshape(source_sum.shape[:-1] + (head_count, HEAD))
    own_sum = jnp.sum(grouped * source_scale[..., None], axis=0)
    attention = (own_sum / own_total[..., None]).reshape(slot_count, token_count, width_local)
    stream = (residual_in.astype(jnp.float32) + attention).astype(jnp.bfloat16)

    block_rows = stream.reshape(slot_count * token_count, width_local)
    full_rows = lax.all_gather(block_rows, "tp", axis=1, tiled=True)
    normed = normalize(full_rows, norm_gain)
    gate_out = jnp.dot(normed, gate_w, preferred_element_type=jnp.float32)
    up_out = jnp.dot(normed, up_w, preferred_element_type=jnp.float32)
    hidden = (jax.nn.silu(gate_out) * up_out).astype(jnp.bfloat16)
    partial_sum = jnp.dot(hidden, down_w, preferred_element_type=jnp.float32)
    unit_share = lax.psum_scatter(
        partial_sum.astype(jnp.bfloat16), "tp", scatter_dimension=1, tiled=True
    ).astype(jnp.float32)
    finished = (block_rows.astype(jnp.float32) + unit_share).astype(jnp.bfloat16)

    owner_ids = owner.reshape(-1)
    owner_count = lax.axis_size(("req", "seq"))
    row_count = owner_ids.shape[0]
    slot_cap = max(2, 2 * row_count // owner_count)
    matches = (owner_ids[:, None] == jnp.arange(owner_count, dtype=jnp.int32)[None, :]).astype(
        jnp.int32
    )
    ranking = jnp.sum(jnp.cumsum(matches, axis=0) * matches, axis=1) - 1
    outgoing = (
        jnp.zeros((owner_count * slot_cap, width_local), jnp.bfloat16)
        .at[owner_ids * slot_cap + ranking]
        .set(finished)
    )
    incoming = lax.all_to_all(
        outgoing.reshape(owner_count, slot_cap, width_local),
        ("req", "seq"),
        split_axis=0,
        concat_axis=0,
        tiled=True,
    )
    return incoming.reshape(1, owner_count, slot_cap, width_local)


def solution(mesh):
    return jax.shard_map(
        per_device,
        mesh=mesh,
        in_specs=(
            P("req", "seq", "tp"),
            P("req", "seq", None, "tp"),
            P("req", "seq", None, "tp"),
            P("req"),
            P("req", "seq", "tp"),
            P(),
            P(None, "tp"),
            P(None, "tp"),
            P("tp", None),
            P(("req", "seq"), None, None),
        ),
        out_specs=P(("req", "seq"), None, None, "tp"),
        check_vma=False,
    )
```

```python
import functools

import jax
import jax.numpy as jnp
from jax import lax
from jax.experimental import pallas as pl
from jax.experimental.pallas import tpu as pltpu
from jax.sharding import PartitionSpec as P

HEAD = 96

masked_floor = -1e30

STAT_LANES = 128
TOTAL_LANE = 8


def attention_kernel(meta_ref, q_ref, kc_ref, vc_ref, kf_ref, vf_ref, out_ref, *, tq, heads):
    slot = pl.program_id(0)
    q_block = pl.program_id(1)
    seq_index = meta_ref[0]
    length = meta_ref[1 + slot]
    span = kc_ref.shape[0]
    fresh_count = kf_ref.shape[0]
    width = q_ref.shape[-1]
    offset = seq_index * span
    scale = HEAD ** (-0.5)

    q = q_ref[...].reshape(tq, q_ref.shape[-1])
    lane = lax.broadcasted_iota(jnp.int32, (1, width), 1)
    stat_lane = lax.broadcasted_iota(jnp.int32, (1, STAT_LANES), 1)
    rows = q_block * tq + lax.broadcasted_iota(jnp.int32, (tq, 1), 0)
    fresh_cols = seq_index * fresh_count + lax.broadcasted_iota(jnp.int32, (1, fresh_count), 1)
    fresh_visible = fresh_cols <= rows
    cached_visible = (offset + lax.broadcasted_iota(jnp.int32, (1, span), 1)) < length
    contract = (((1,), (1,)), ((), ()))

    def run(with_cache):
        kf = kf_ref[...]
        vf = vf_ref[...]
        if with_cache:
            kc = kc_ref[...]
            vc = vc_ref[...]
        weighted = jnp.zeros((tq, width), jnp.float32)
        stats = jnp.zeros((tq, STAT_LANES), jnp.float32)
        for h in range(heads):
            head_lanes = (lane >= h * HEAD) & (lane < (h + 1) * HEAD)
            qh = jnp.where(head_lanes, q, jnp.zeros_like(q))
            sf = lax.dot_general(qh, kf, contract, preferred_element_type=jnp.float32) * scale
            sf = jnp.where(fresh_visible, sf, masked_floor)
            peak = jnp.max(sf, axis=-1, keepdims=True)
            if with_cache:
                sc = lax.dot_general(qh, kc, contract, preferred_element_type=jnp.float32) * scale
                sc = jnp.where(cached_visible, sc, masked_floor)
                peak = jnp.maximum(peak, jnp.max(sc, axis=-1, keepdims=True))
            pf = jnp.where(fresh_visible, jnp.exp(sf - peak), 0.0)
            total = jnp.sum(pf, axis=-1, keepdims=True)
            oh = jnp.dot(pf.astype(jnp.bfloat16), vf, preferred_element_type=jnp.float32)
            if with_cache:
                pc = jnp.where(cached_visible, jnp.exp(sc - peak), 0.0)
                total = total + jnp.sum(pc, axis=-1, keepdims=True)
                oh = oh + jnp.dot(pc.astype(jnp.bfloat16), vc, preferred_element_type=jnp.float32)
            weighted = jnp.where(head_lanes, oh, weighted)
            stats = jnp.where(stat_lane == h, peak, stats)
            stats = jnp.where(stat_lane == TOTAL_LANE + h, total, stats)
        out_ref[:, :width] = weighted
        out_ref[:, width:] = stats

    @pl.when(offset < length)
    def _():
        run(True)

    @pl.when(offset >= length)
    def _():
        run(False)


def local_attention(all_queries, cache_kv, new_kv, cached_len, seq_index):
    source_count, slot_count, token_count, width = all_queries.shape
    query_count = source_count * token_count
    span = cache_kv.shape[1]
    fresh_count = new_kv.shape[1]
    heads = width // HEAD
    tq = 256 if query_count % 256 == 0 else query_count
    cache2 = cache_kv.reshape(slot_count, span, 2 * width)
    fresh2 = new_kv.reshape(slot_count, fresh_count, 2 * width)
    meta = jnp.concatenate([jnp.reshape(seq_index, (1,)).astype(jnp.int32), cached_len.astype(jnp.int32)])
    kernel = functools.partial(attention_kernel, tq=tq, heads=heads)
    grid_spec = pltpu.PrefetchScalarGridSpec(
        num_scalar_prefetch=1,
        grid=(slot_count, query_count // tq),
        in_specs=[
            pl.BlockSpec((tq // token_count, None, token_count, width), lambda s, b, m: (b, s, 0, 0)),
            pl.BlockSpec((None, span, width), lambda s, b, m: (s, 0, 0)),
            pl.BlockSpec((None, span, width), lambda s, b, m: (s, 0, 1)),
            pl.BlockSpec((None, fresh_count, width), lambda s, b, m: (s, 0, 0)),
            pl.BlockSpec((None, fresh_count, width), lambda s, b, m: (s, 0, 1)),
        ],
        out_specs=pl.BlockSpec((None, tq, width + STAT_LANES), lambda s, b, m: (s, b, 0)),
    )
    return pl.pallas_call(
        kernel,
        grid_spec=grid_spec,
        out_shape=jax.ShapeDtypeStruct((slot_count, query_count, width + STAT_LANES), jnp.float32),
    )(meta, all_queries, cache2, cache2, fresh2, fresh2)


def normalize(features, norm_gain):
    values = features.astype(jnp.float32)
    mean_square = jnp.mean(values * values, axis=-1, keepdims=True)
    return (values * lax.rsqrt(mean_square + 1e-05) * norm_gain).astype(jnp.bfloat16)


def per_device(
    queries, new_kv, cache_kv, cached_len, residual_in, norm_gain, gate_w, up_w, down_w, owner
):
    slot_count, token_count, width_local = queries.shape
    head_count = width_local // HEAD
    seq_index = lax.axis_index("seq")
    seq_count = lax.axis_size("seq")
    all_queries = lax.all_to_all(
        jnp.broadcast_to(queries[None], (seq_count,) + queries.shape), "seq", 0, 0, tiled=True
    )
    packed = local_attention(all_queries, cache_kv, new_kv, cached_len, seq_index)
    source = lax.all_to_all(packed[None], "seq", split_axis=2, concat_axis=0, tiled=True)
    source_sum = source[..., :width_local]
    source_peak = source[..., width_local:width_local + head_count]
    source_total = source[..., width_local + TOTAL_LANE:width_local + TOTAL_LANE + head_count]
    joint_peak = jnp.max(source_peak, axis=0)
    source_scale = jnp.exp(source_peak - joint_peak[None])
    own_total = jnp.sum(source_total * source_scale, axis=0)
    grouped = source_sum.reshape(source_sum.shape[:-1] + (head_count, HEAD))
    own_sum = jnp.sum(grouped * source_scale[..., None], axis=0)
    attention = (own_sum / own_total[..., None]).reshape(slot_count, token_count, width_local)
    stream = (residual_in.astype(jnp.float32) + attention).astype(jnp.bfloat16)

    block_rows = stream.reshape(slot_count * token_count, width_local)
    tp_count = lax.axis_size("tp")
    row_count = block_rows.shape[0]
    full_rows = (
        lax.all_to_all(
            jnp.broadcast_to(block_rows[None], (tp_count,) + block_rows.shape), "tp", 0, 0, tiled=True
        )
        .transpose(1, 0, 2)
        .reshape(row_count, tp_count * width_local)
    )
    normed = normalize(full_rows, norm_gain)
    gate_out = jnp.dot(normed, gate_w, preferred_element_type=jnp.float32)
    up_out = jnp.dot(normed, up_w, preferred_element_type=jnp.float32)
    hidden = (jax.nn.silu(gate_out) * up_out).astype(jnp.bfloat16)
    partial_sum = jnp.dot(hidden, down_w, preferred_element_type=jnp.float32)
    pieces = partial_sum.astype(jnp.bfloat16).reshape(row_count, tp_count, width_local).transpose(1, 0, 2)
    unit_share = jnp.sum(
        lax.all_to_all(pieces, "tp", 0, 0, tiled=True).astype(jnp.float32), axis=0
    )
    finished = (block_rows.astype(jnp.float32) + unit_share).astype(jnp.bfloat16)

    owner_ids = owner.reshape(-1)
    owner_count = lax.axis_size(("req", "seq"))
    slot_cap = max(2, 2 * row_count // owner_count)
    matches = (owner_ids[:, None] == jnp.arange(owner_count, dtype=jnp.int32)[None, :]).astype(
        jnp.int32
    )
    ranking = jnp.sum(jnp.cumsum(matches, axis=0) * matches, axis=1) - 1
    outgoing = (
        jnp.zeros((owner_count * slot_cap, width_local), jnp.bfloat16)
        .at[owner_ids * slot_cap + ranking]
        .set(finished)
    )
    incoming = lax.all_to_all(
        outgoing.reshape(owner_count, slot_cap, width_local),
        ("req", "seq"),
        split_axis=0,
        concat_axis=0,
        tiled=True,
    )
    return incoming.reshape(1, owner_count, slot_cap, width_local)


def solution(mesh):
    return jax.shard_map(
        per_device,
        mesh=mesh,
        in_specs=(
            P("req", "seq", "tp"),
            P("req", "seq", None, "tp"),
            P("req", "seq", None, "tp"),
            P("req"),
            P("req", "seq", "tp"),
            P(),
            P(None, "tp"),
            P(None, "tp"),
            P("tp", None),
            P(("req", "seq"), None, None),
        ),
        out_specs=P(("req", "seq"), None, None, "tp"),
        check_vma=False,
    )
```

```python
import functools

import jax
import jax.numpy as jnp
from jax import lax
from jax.experimental import pallas as pl
from jax.experimental.pallas import tpu as pltpu
from jax.sharding import PartitionSpec as P

HEAD = 96

masked_floor = -1e30


def attention_kernel(meta_ref, q_ref, kc_ref, vc_ref, kf_ref, vf_ref, sum_ref, stat_ref, *, tq, heads):
    slot = pl.program_id(0)
    q_block = pl.program_id(1)
    seq_index = meta_ref[0]
    length = meta_ref[1 + slot]
    span = kc_ref.shape[0]
    fresh_count = kf_ref.shape[0]
    width = q_ref.shape[-1]
    offset = seq_index * span
    scale = HEAD ** (-0.5)

    q = q_ref[...].reshape(tq, q_ref.shape[-1])
    lane = lax.broadcasted_iota(jnp.int32, (1, width), 1)
    stat_lane = lax.broadcasted_iota(jnp.int32, (1, 2 * heads), 1)
    rows = q_block * tq + lax.broadcasted_iota(jnp.int32, (tq, 1), 0)
    fresh_cols = seq_index * fresh_count + lax.broadcasted_iota(jnp.int32, (1, fresh_count), 1)
    fresh_visible = fresh_cols <= rows
    cached_visible = (offset + lax.broadcasted_iota(jnp.int32, (1, span), 1)) < length
    contract = (((1,), (1,)), ((), ()))

    def run(with_cache):
        kf = kf_ref[...]
        vf = vf_ref[...]
        if with_cache:
            kc = kc_ref[...]
            vc = vc_ref[...]
        weighted = jnp.zeros((tq, width), jnp.float32)
        stats = jnp.zeros((tq, 2 * heads), jnp.float32)
        for h in range(heads):
            head_lanes = (lane >= h * HEAD) & (lane < (h + 1) * HEAD)
            qh = jnp.where(head_lanes, q, jnp.zeros_like(q))
            sf = lax.dot_general(qh, kf, contract, preferred_element_type=jnp.float32) * scale
            sf = jnp.where(fresh_visible, sf, masked_floor)
            peak = jnp.max(sf, axis=-1, keepdims=True)
            if with_cache:
                sc = lax.dot_general(qh, kc, contract, preferred_element_type=jnp.float32) * scale
                sc = jnp.where(cached_visible, sc, masked_floor)
                peak = jnp.maximum(peak, jnp.max(sc, axis=-1, keepdims=True))
            pf = jnp.where(fresh_visible, jnp.exp(sf - peak), 0.0)
            total = jnp.sum(pf, axis=-1, keepdims=True)
            oh = jnp.dot(pf.astype(jnp.bfloat16), vf, preferred_element_type=jnp.float32)
            if with_cache:
                pc = jnp.where(cached_visible, jnp.exp(sc - peak), 0.0)
                total = total + jnp.sum(pc, axis=-1, keepdims=True)
                oh = oh + jnp.dot(pc.astype(jnp.bfloat16), vc, preferred_element_type=jnp.float32)
            weighted = jnp.where(head_lanes, oh, weighted)
            stats = jnp.where(stat_lane == h, peak, stats)
            stats = jnp.where(stat_lane == heads + h, total, stats)
        sum_ref[...] = weighted.astype(sum_ref.dtype)
        stat_ref[...] = stats

    @pl.when(offset < length)
    def _():
        run(True)

    @pl.when(offset >= length)
    def _():
        run(False)


def local_attention(all_queries, cache_kv, new_kv, cached_len, seq_index):
    source_count, slot_count, token_count, width = all_queries.shape
    query_count = source_count * token_count
    span = cache_kv.shape[1]
    fresh_count = new_kv.shape[1]
    heads = width // HEAD
    tq = 256 if query_count % 256 == 0 else query_count
    cache2 = cache_kv.reshape(slot_count, span, 2 * width)
    fresh2 = new_kv.reshape(slot_count, fresh_count, 2 * width)
    meta = jnp.concatenate([jnp.reshape(seq_index, (1,)).astype(jnp.int32), cached_len.astype(jnp.int32)])
    kernel = functools.partial(attention_kernel, tq=tq, heads=heads)
    grid_spec = pltpu.PrefetchScalarGridSpec(
        num_scalar_prefetch=1,
        grid=(slot_count, query_count // tq),
        in_specs=[
            pl.BlockSpec((tq // token_count, None, token_count, width), lambda s, b, m: (b, s, 0, 0)),
            pl.BlockSpec((None, span, width), lambda s, b, m: (s, 0, 0)),
            pl.BlockSpec((None, span, width), lambda s, b, m: (s, 0, 1)),
            pl.BlockSpec((None, fresh_count, width), lambda s, b, m: (s, 0, 0)),
            pl.BlockSpec((None, fresh_count, width), lambda s, b, m: (s, 0, 1)),
        ],
        out_specs=[
            pl.BlockSpec((None, tq, width), lambda s, b, m: (s, b, 0)),
            pl.BlockSpec((None, tq, 2 * heads), lambda s, b, m: (s, b, 0)),
        ],
    )
    return pl.pallas_call(
        kernel,
        grid_spec=grid_spec,
        out_shape=[
            jax.ShapeDtypeStruct((slot_count, query_count, width), jnp.bfloat16),
            jax.ShapeDtypeStruct((slot_count, query_count, 2 * heads), jnp.float32),
        ],
    )(meta, all_queries, cache2, cache2, fresh2, fresh2)


def combine_kernel(sum_ref, stat_ref, residual_ref, out_ref, *, heads):
    stats = stat_ref[...]
    sums = sum_ref[...].astype(jnp.float32)
    width = sums.shape[-1]
    lane = lax.broadcasted_iota(jnp.int32, (1, width), 1)
    attention = jnp.zeros(sums.shape[1:], jnp.float32)
    for h in range(heads):
        peak = stats[:, :, h:h + 1]
        joint_peak = jnp.max(peak, axis=0)
        scale = jnp.exp(peak - joint_peak[None])
        total = jnp.sum(stats[:, :, heads + h:heads + h + 1] * scale, axis=0)
        head_sum = jnp.sum(sums * scale, axis=0)
        head_lanes = (lane >= h * HEAD) & (lane < (h + 1) * HEAD)
        attention = jnp.where(head_lanes, head_sum / total, attention)
    out_ref[...] = (residual_ref[...].astype(jnp.float32) + attention).astype(out_ref.dtype)


def combine(source_sum, source_stats, residual_rows):
    heads = source_stats.shape[-1] // 2
    return pl.pallas_call(
        functools.partial(combine_kernel, heads=heads),
        out_shape=jax.ShapeDtypeStruct(residual_rows.shape, jnp.bfloat16),
    )(source_sum, source_stats, residual_rows)


def normalize(features, norm_gain):
    values = features.astype(jnp.float32)
    mean_square = jnp.mean(values * values, axis=-1, keepdims=True)
    return (values * lax.rsqrt(mean_square + 1e-05) * norm_gain).astype(jnp.bfloat16)


def per_device(
    queries, new_kv, cache_kv, cached_len, residual_in, norm_gain, gate_w, up_w, down_w, owner
):
    slot_count, token_count, width_local = queries.shape
    head_count = width_local // HEAD
    seq_index = lax.axis_index("seq")
    seq_count = lax.axis_size("seq")
    all_queries = lax.all_to_all(
        jnp.broadcast_to(queries[None], (seq_count,) + queries.shape), "seq", 0, 0, tiled=True
    )
    partial_sum, partial_stats = local_attention(all_queries, cache_kv, new_kv, cached_len, seq_index)
    source_sum = lax.all_to_all(partial_sum[None], "seq", split_axis=2, concat_axis=0, tiled=True)
    source_stats = lax.all_to_all(partial_stats[None], "seq", split_axis=2, concat_axis=0, tiled=True)
    row_count = slot_count * token_count
    block_rows = combine(
        source_sum.reshape(seq_count, row_count, width_local),
        source_stats.reshape(seq_count, row_count, 2 * head_count),
        residual_in.reshape(row_count, width_local),
    )
    tp_count = lax.axis_size("tp")
    full_rows = (
        lax.all_to_all(
            jnp.broadcast_to(block_rows[None], (tp_count,) + block_rows.shape), "tp", 0, 0, tiled=True
        )
        .transpose(1, 0, 2)
        .reshape(row_count, tp_count * width_local)
    )
    normed = normalize(full_rows, norm_gain)
    gate_out = jnp.dot(normed, gate_w, preferred_element_type=jnp.float32)
    up_out = jnp.dot(normed, up_w, preferred_element_type=jnp.float32)
    hidden = (jax.nn.silu(gate_out) * up_out).astype(jnp.bfloat16)
    partial_sum = jnp.dot(hidden, down_w, preferred_element_type=jnp.float32)
    pieces = partial_sum.astype(jnp.bfloat16).reshape(row_count, tp_count, width_local).transpose(1, 0, 2)
    unit_share = jnp.sum(
        lax.all_to_all(pieces, "tp", 0, 0, tiled=True).astype(jnp.float32), axis=0
    )
    finished = (block_rows.astype(jnp.float32) + unit_share).astype(jnp.bfloat16)

    owner_ids = owner.reshape(-1)
    owner_count = lax.axis_size(("req", "seq"))
    slot_cap = max(2, 2 * row_count // owner_count)
    matches = (owner_ids[:, None] == jnp.arange(owner_count, dtype=jnp.int32)[None, :]).astype(
        jnp.int32
    )
    ranking = jnp.sum(jnp.cumsum(matches, axis=0) * matches, axis=1) - 1
    outgoing = (
        jnp.zeros((owner_count * slot_cap, width_local), jnp.bfloat16)
        .at[owner_ids * slot_cap + ranking]
        .set(finished)
    )
    incoming = lax.all_to_all(
        outgoing.reshape(owner_count, slot_cap, width_local),
        ("req", "seq"),
        split_axis=0,
        concat_axis=0,
        tiled=True,
    )
    return incoming.reshape(1, owner_count, slot_cap, width_local)


def solution(mesh):
    return jax.shard_map(
        per_device,
        mesh=mesh,
        in_specs=(
            P("req", "seq", "tp"),
            P("req", "seq", None, "tp"),
            P("req", "seq", None, "tp"),
            P("req"),
            P("req", "seq", "tp"),
            P(),
            P(None, "tp"),
            P(None, "tp"),
            P("tp", None),
            P(("req", "seq"), None, None),
        ),
        out_specs=P(("req", "seq"), None, None, "tp"),
        check_vma=False,
    )
```

```python
import functools

import jax
import jax.numpy as jnp
from jax import lax
from jax.experimental import pallas as pl
from jax.experimental.pallas import tpu as pltpu
from jax.sharding import PartitionSpec as P

HEAD = 96

masked_floor = -1e30


def attention_kernel(meta_ref, q_ref, kc_ref, vc_ref, kf_ref, vf_ref, sum_ref, stat_ref, *, tq, heads):
    slot = pl.program_id(0)
    q_block = pl.program_id(1)
    seq_index = meta_ref[0]
    length = meta_ref[1 + slot]
    span = kc_ref.shape[0]
    fresh_count = kf_ref.shape[0]
    width = q_ref.shape[-1]
    offset = seq_index * span
    scale = HEAD ** (-0.5)

    q = q_ref[...].reshape(tq, q_ref.shape[-1])
    lane = lax.broadcasted_iota(jnp.int32, (1, width), 1)
    stat_lane = lax.broadcasted_iota(jnp.int32, (1, 2 * heads), 1)
    rows = q_block * tq + lax.broadcasted_iota(jnp.int32, (tq, 1), 0)
    fresh_cols = seq_index * fresh_count + lax.broadcasted_iota(jnp.int32, (1, fresh_count), 1)
    fresh_visible = fresh_cols <= rows
    cached_visible = (offset + lax.broadcasted_iota(jnp.int32, (1, span), 1)) < length
    contract = (((1,), (1,)), ((), ()))

    def run(with_cache):
        kf = kf_ref[...]
        vf = vf_ref[...]
        if with_cache:
            kc = kc_ref[...]
            vc = vc_ref[...]
        weighted = jnp.zeros((tq, width), jnp.float32)
        stats = jnp.zeros((tq, 2 * heads), jnp.float32)
        for h in range(heads):
            head_lanes = (lane >= h * HEAD) & (lane < (h + 1) * HEAD)
            qh = jnp.where(head_lanes, q, jnp.zeros_like(q))
            sf = lax.dot_general(qh, kf, contract, preferred_element_type=jnp.float32) * scale
            sf = jnp.where(fresh_visible, sf, masked_floor)
            peak = jnp.max(sf, axis=-1, keepdims=True)
            if with_cache:
                sc = lax.dot_general(qh, kc, contract, preferred_element_type=jnp.float32) * scale
                sc = jnp.where(cached_visible, sc, masked_floor)
                peak = jnp.maximum(peak, jnp.max(sc, axis=-1, keepdims=True))
            pf = jnp.where(fresh_visible, jnp.exp(sf - peak), 0.0)
            total = jnp.sum(pf, axis=-1, keepdims=True)
            oh = jnp.dot(pf.astype(jnp.bfloat16), vf, preferred_element_type=jnp.float32)
            if with_cache:
                pc = jnp.where(cached_visible, jnp.exp(sc - peak), 0.0)
                total = total + jnp.sum(pc, axis=-1, keepdims=True)
                oh = oh + jnp.dot(pc.astype(jnp.bfloat16), vc, preferred_element_type=jnp.float32)
            weighted = jnp.where(head_lanes, oh, weighted)
            stats = jnp.where(stat_lane == h, peak, stats)
            stats = jnp.where(stat_lane == heads + h, total, stats)
        sum_ref[...] = weighted.reshape(sum_ref.shape).astype(sum_ref.dtype)
        stat_ref[...] = stats.reshape(stat_ref.shape)

    @pl.when(offset < length)
    def _():
        run(True)

    @pl.when(offset >= length)
    def _():
        run(False)


def local_attention(all_queries, cache_kv, new_kv, cached_len, seq_index):
    source_count, slot_count, token_count, width = all_queries.shape
    query_count = source_count * token_count
    span = cache_kv.shape[1]
    fresh_count = new_kv.shape[1]
    heads = width // HEAD
    tq = 256 if query_count % 256 == 0 else query_count
    cache2 = cache_kv.reshape(slot_count, span, 2 * width)
    fresh2 = new_kv.reshape(slot_count, fresh_count, 2 * width)
    meta = jnp.concatenate([jnp.reshape(seq_index, (1,)).astype(jnp.int32), cached_len.astype(jnp.int32)])
    kernel = functools.partial(attention_kernel, tq=tq, heads=heads)
    grid_spec = pltpu.PrefetchScalarGridSpec(
        num_scalar_prefetch=1,
        grid=(slot_count, query_count // tq),
        in_specs=[
            pl.BlockSpec((tq // token_count, None, token_count, width), lambda s, b, m: (b, s, 0, 0)),
            pl.BlockSpec((None, span, width), lambda s, b, m: (s, 0, 0)),
            pl.BlockSpec((None, span, width), lambda s, b, m: (s, 0, 1)),
            pl.BlockSpec((None, fresh_count, width), lambda s, b, m: (s, 0, 0)),
            pl.BlockSpec((None, fresh_count, width), lambda s, b, m: (s, 0, 1)),
        ],
        out_specs=[
            pl.BlockSpec((tq // token_count, None, token_count, width), lambda s, b, m: (b, s, 0, 0)),
            pl.BlockSpec((tq // token_count, None, token_count, 2 * heads), lambda s, b, m: (b, s, 0, 0)),
        ],
    )
    return pl.pallas_call(
        kernel,
        grid_spec=grid_spec,
        out_shape=[
            jax.ShapeDtypeStruct((source_count, slot_count, token_count, width), jnp.bfloat16),
            jax.ShapeDtypeStruct((source_count, slot_count, token_count, 2 * heads), jnp.float32),
        ],
    )(meta, all_queries, cache2, cache2, fresh2, fresh2)


def combine_kernel(sum_ref, stat_ref, residual_ref, out_ref, *, heads):
    stats = stat_ref[...]
    sums = sum_ref[...].astype(jnp.float32)
    width = sums.shape[-1]
    lane = lax.broadcasted_iota(jnp.int32, (1, width), 1)
    attention = jnp.zeros(sums.shape[1:], jnp.float32)
    for h in range(heads):
        peak = stats[:, :, h:h + 1]
        joint_peak = jnp.max(peak, axis=0)
        scale = jnp.exp(peak - joint_peak[None])
        total = jnp.sum(stats[:, :, heads + h:heads + h + 1] * scale, axis=0)
        head_sum = jnp.sum(sums * scale, axis=0)
        head_lanes = (lane >= h * HEAD) & (lane < (h + 1) * HEAD)
        attention = jnp.where(head_lanes, head_sum / total, attention)
    out_ref[...] = (residual_ref[...].astype(jnp.float32) + attention).astype(out_ref.dtype)


def combine(source_sum, source_stats, residual_rows):
    heads = source_stats.shape[-1] // 2
    return pl.pallas_call(
        functools.partial(combine_kernel, heads=heads),
        out_shape=jax.ShapeDtypeStruct(residual_rows.shape, jnp.bfloat16),
    )(source_sum, source_stats, residual_rows)


def normalize(features, norm_gain):
    values = features.astype(jnp.float32)
    mean_square = jnp.mean(values * values, axis=-1, keepdims=True)
    return (values * lax.rsqrt(mean_square + 1e-05) * norm_gain).astype(jnp.bfloat16)


def per_device(
    queries, new_kv, cache_kv, cached_len, residual_in, norm_gain, gate_w, up_w, down_w, owner
):
    slot_count, token_count, width_local = queries.shape
    head_count = width_local // HEAD
    seq_index = lax.axis_index("seq")
    seq_count = lax.axis_size("seq")
    all_queries = lax.all_to_all(
        jnp.broadcast_to(queries[None], (seq_count,) + queries.shape), "seq", 0, 0, tiled=True
    )
    partial_sum, partial_stats = local_attention(all_queries, cache_kv, new_kv, cached_len, seq_index)
    source_sum = lax.all_to_all(partial_sum, "seq", 0, 0, tiled=True)
    source_stats = lax.all_to_all(partial_stats, "seq", 0, 0, tiled=True)
    row_count = slot_count * token_count
    block_rows = combine(
        source_sum.reshape(seq_count, row_count, width_local),
        source_stats.reshape(seq_count, row_count, 2 * head_count),
        residual_in.reshape(row_count, width_local),
    )
    tp_count = lax.axis_size("tp")
    full_rows = (
        lax.all_to_all(
            jnp.broadcast_to(block_rows[None], (tp_count,) + block_rows.shape), "tp", 0, 0, tiled=True
        )
        .transpose(1, 0, 2)
        .reshape(row_count, tp_count * width_local)
    )
    normed = normalize(full_rows, norm_gain)
    gate_out = jnp.dot(normed, gate_w, preferred_element_type=jnp.float32)
    up_out = jnp.dot(normed, up_w, preferred_element_type=jnp.float32)
    hidden = (jax.nn.silu(gate_out) * up_out).astype(jnp.bfloat16)
    partial_sum = jnp.dot(hidden, down_w, preferred_element_type=jnp.float32)
    pieces = partial_sum.astype(jnp.bfloat16).reshape(row_count, tp_count, width_local).transpose(1, 0, 2)
    unit_share = jnp.sum(
        lax.all_to_all(pieces, "tp", 0, 0, tiled=True).astype(jnp.float32), axis=0
    )
    finished = (block_rows.astype(jnp.float32) + unit_share).astype(jnp.bfloat16)

    owner_ids = owner.reshape(-1)
    owner_count = lax.axis_size(("req", "seq"))
    slot_cap = max(2, 2 * row_count // owner_count)
    matches = (owner_ids[:, None] == jnp.arange(owner_count, dtype=jnp.int32)[None, :]).astype(
        jnp.int32
    )
    ranking = jnp.sum(jnp.cumsum(matches, axis=0) * matches, axis=1) - 1
    outgoing = (
        jnp.zeros((owner_count * slot_cap, width_local), jnp.bfloat16)
        .at[owner_ids * slot_cap + ranking]
        .set(finished)
    )
    incoming = lax.all_to_all(
        outgoing.reshape(owner_count, slot_cap, width_local),
        ("req", "seq"),
        split_axis=0,
        concat_axis=0,
        tiled=True,
    )
    return incoming.reshape(1, owner_count, slot_cap, width_local)


def solution(mesh):
    return jax.shard_map(
        per_device,
        mesh=mesh,
        in_specs=(
            P("req", "seq", "tp"),
            P("req", "seq", None, "tp"),
            P("req", "seq", None, "tp"),
            P("req"),
            P("req", "seq", "tp"),
            P(),
            P(None, "tp"),
            P(None, "tp"),
            P("tp", None),
            P(("req", "seq"), None, None),
        ),
        out_specs=P(("req", "seq"), None, None, "tp"),
        check_vma=False,
    )
```

```python
import functools

import jax
import jax.numpy as jnp
from jax import lax
from jax.experimental import pallas as pl
from jax.experimental.pallas import tpu as pltpu
from jax.sharding import PartitionSpec as P

HEAD = 96

masked_floor = -1e30
LANE = 128


def attention_kernel(meta_ref, q_ref, kc_ref, vc_ref, kf_ref, vf_ref, sum_ref, stat_ref, *, tq, heads):
    slot = pl.program_id(0)
    q_block = pl.program_id(1)
    seq_index = meta_ref[0]
    length = meta_ref[1 + slot]
    span = kc_ref.shape[0]
    fresh_count = kf_ref.shape[0]
    width = q_ref.shape[-1]
    offset = seq_index * span
    scale = HEAD ** (-0.5)

    q = q_ref[...].reshape(tq, q_ref.shape[-1])
    lane = lax.broadcasted_iota(jnp.int32, (1, width), 1)
    stat_lane = lax.broadcasted_iota(jnp.int32, (1, 2 * heads), 1)
    rows = q_block * tq + lax.broadcasted_iota(jnp.int32, (tq, 1), 0)
    fresh_cols = seq_index * fresh_count + lax.broadcasted_iota(jnp.int32, (1, fresh_count), 1)
    fresh_visible = fresh_cols <= rows
    cached_visible = (offset + lax.broadcasted_iota(jnp.int32, (1, span), 1)) < length
    contract = (((1,), (1,)), ((), ()))

    def run(with_cache):
        kf = kf_ref[...]
        vf = vf_ref[...]
        if with_cache:
            kc = kc_ref[...]
            vc = vc_ref[...]
        tiles = [jnp.zeros((tq, LANE), jnp.float32) for _ in range(width // LANE)]
        stats = jnp.zeros((tq, 2 * heads), jnp.float32)
        for h in range(heads):
            lo = h * HEAD // LANE * LANE
            hi = -(-(h + 1) * HEAD // LANE) * LANE
            head_lanes = (lane >= h * HEAD) & (lane < (h + 1) * HEAD)
            qh = jnp.where(head_lanes[:, lo:hi], q[:, lo:hi], jnp.zeros_like(q[:, lo:hi]))
            sf = lax.dot_general(qh, kf[:, lo:hi], contract, preferred_element_type=jnp.float32)
            sf = jnp.where(fresh_visible, sf, masked_floor)
            peak = jnp.max(sf, axis=-1, keepdims=True)
            if with_cache:
                sc = lax.dot_general(qh, kc[:, lo:hi], contract, preferred_element_type=jnp.float32)
                sc = jnp.where(cached_visible, sc, masked_floor)
                peak = jnp.maximum(peak, jnp.max(sc, axis=-1, keepdims=True))
            pf = jnp.where(fresh_visible, jnp.exp((sf - peak) * scale), 0.0)
            total = jnp.sum(pf, axis=-1, keepdims=True)
            oh = jnp.dot(pf.astype(jnp.bfloat16), vf[:, lo:hi], preferred_element_type=jnp.float32)
            if with_cache:
                pc = jnp.exp((sc - peak) * scale)
                total = total + jnp.sum(pc, axis=-1, keepdims=True)
                oh = oh + jnp.dot(pc.astype(jnp.bfloat16), vc[:, lo:hi], preferred_element_type=jnp.float32)
            for j in range(lo // LANE, hi // LANE):
                part = oh[:, j * LANE - lo:(j + 1) * LANE - lo]
                tiles[j] = jnp.where(head_lanes[:, j * LANE:(j + 1) * LANE], part, tiles[j])
            stats = jnp.where(stat_lane == h, peak * scale, stats)
            stats = jnp.where(stat_lane == heads + h, total, stats)
        weighted = jnp.concatenate(tiles, axis=1)
        sum_ref[...] = weighted.reshape(sum_ref.shape).astype(sum_ref.dtype)
        stat_ref[...] = stats.reshape(stat_ref.shape)

    @pl.when(offset < length)
    def _():
        run(True)

    @pl.when(offset >= length)
    def _():
        run(False)


def local_attention(all_queries, cache_kv, new_kv, cached_len, seq_index):
    source_count, slot_count, token_count, width = all_queries.shape
    query_count = source_count * token_count
    span = cache_kv.shape[1]
    fresh_count = new_kv.shape[1]
    heads = width // HEAD
    tq = 256 if query_count % 256 == 0 else query_count
    cache2 = cache_kv.reshape(slot_count, span, 2 * width)
    fresh2 = new_kv.reshape(slot_count, fresh_count, 2 * width)
    meta = jnp.concatenate([jnp.reshape(seq_index, (1,)).astype(jnp.int32), cached_len.astype(jnp.int32)])
    kernel = functools.partial(attention_kernel, tq=tq, heads=heads)
    grid_spec = pltpu.PrefetchScalarGridSpec(
        num_scalar_prefetch=1,
        grid=(slot_count, query_count // tq),
        in_specs=[
            pl.BlockSpec((tq // token_count, None, token_count, width), lambda s, b, m: (b, s, 0, 0)),
            pl.BlockSpec((None, span, width), lambda s, b, m: (s, 0, 0)),
            pl.BlockSpec((None, span, width), lambda s, b, m: (s, 0, 1)),
            pl.BlockSpec((None, fresh_count, width), lambda s, b, m: (s, 0, 0)),
            pl.BlockSpec((None, fresh_count, width), lambda s, b, m: (s, 0, 1)),
        ],
        out_specs=[
            pl.BlockSpec((tq // token_count, None, token_count, width), lambda s, b, m: (b, s, 0, 0)),
            pl.BlockSpec((tq // token_count, None, token_count, 2 * heads), lambda s, b, m: (b, s, 0, 0)),
        ],
    )
    return pl.pallas_call(
        kernel,
        grid_spec=grid_spec,
        out_shape=[
            jax.ShapeDtypeStruct((source_count, slot_count, token_count, width), jnp.bfloat16),
            jax.ShapeDtypeStruct((source_count, slot_count, token_count, 2 * heads), jnp.float32),
        ],
    )(meta, all_queries, cache2, cache2, fresh2, fresh2)


def combine_kernel(sum_ref, stat_ref, residual_ref, out_ref, *, heads):
    stats = stat_ref[...]
    sums = sum_ref[...].astype(jnp.float32)
    width = sums.shape[-1]
    lane = lax.broadcasted_iota(jnp.int32, (1, width), 1)
    attention = jnp.zeros(sums.shape[1:], jnp.float32)
    for h in range(heads):
        peak = stats[:, :, h:h + 1]
        joint_peak = jnp.max(peak, axis=0)
        scale = jnp.exp(peak - joint_peak[None])
        total = jnp.sum(stats[:, :, heads + h:heads + h + 1] * scale, axis=0)
        head_sum = jnp.sum(sums * scale, axis=0)
        head_lanes = (lane >= h * HEAD) & (lane < (h + 1) * HEAD)
        attention = jnp.where(head_lanes, head_sum / total, attention)
    out_ref[...] = (residual_ref[...].astype(jnp.float32) + attention).astype(out_ref.dtype)


def combine(source_sum, source_stats, residual_rows):
    heads = source_stats.shape[-1] // 2
    return pl.pallas_call(
        functools.partial(combine_kernel, heads=heads),
        out_shape=jax.ShapeDtypeStruct(residual_rows.shape, jnp.bfloat16),
    )(source_sum, source_stats, residual_rows)


def normalize(features, norm_gain):
    values = features.astype(jnp.float32)
    mean_square = jnp.mean(values * values, axis=-1, keepdims=True)
    return (values * lax.rsqrt(mean_square + 1e-05) * norm_gain).astype(jnp.bfloat16)


def per_device(
    queries, new_kv, cache_kv, cached_len, residual_in, norm_gain, gate_w, up_w, down_w, owner
):
    slot_count, token_count, width_local = queries.shape
    head_count = width_local // HEAD
    seq_index = lax.axis_index("seq")
    seq_count = lax.axis_size("seq")
    all_queries = lax.all_to_all(
        jnp.broadcast_to(queries[None], (seq_count,) + queries.shape), "seq", 0, 0, tiled=True
    )
    partial_sum, partial_stats = local_attention(all_queries, cache_kv, new_kv, cached_len, seq_index)
    source_sum = lax.all_to_all(partial_sum, "seq", 0, 0, tiled=True)
    source_stats = lax.all_to_all(partial_stats, "seq", 0, 0, tiled=True)
    row_count = slot_count * token_count
    block_rows = combine(
        source_sum.reshape(seq_count, row_count, width_local),
        source_stats.reshape(seq_count, row_count, 2 * head_count),
        residual_in.reshape(row_count, width_local),
    )
    tp_count = lax.axis_size("tp")
    full_rows = (
        lax.all_to_all(
            jnp.broadcast_to(block_rows[None], (tp_count,) + block_rows.shape), "tp", 0, 0, tiled=True
        )
        .transpose(1, 0, 2)
        .reshape(row_count, tp_count * width_local)
    )
    normed = normalize(full_rows, norm_gain)
    gate_out = jnp.dot(normed, gate_w, preferred_element_type=jnp.float32)
    up_out = jnp.dot(normed, up_w, preferred_element_type=jnp.float32)
    hidden = (jax.nn.silu(gate_out) * up_out).astype(jnp.bfloat16)
    partial_sum = jnp.dot(hidden, down_w, preferred_element_type=jnp.float32)
    pieces = partial_sum.astype(jnp.bfloat16).reshape(row_count, tp_count, width_local).transpose(1, 0, 2)
    unit_share = jnp.sum(
        lax.all_to_all(pieces, "tp", 0, 0, tiled=True).astype(jnp.float32), axis=0
    )
    finished = (block_rows.astype(jnp.float32) + unit_share).astype(jnp.bfloat16)

    owner_ids = owner.reshape(-1)
    owner_count = lax.axis_size(("req", "seq"))
    slot_cap = max(2, 2 * row_count // owner_count)
    matches = (owner_ids[:, None] == jnp.arange(owner_count, dtype=jnp.int32)[None, :]).astype(
        jnp.int32
    )
    ranking = jnp.sum(jnp.cumsum(matches, axis=0) * matches, axis=1) - 1
    outgoing = (
        jnp.zeros((owner_count * slot_cap, width_local), jnp.bfloat16)
        .at[owner_ids * slot_cap + ranking]
        .set(finished)
    )
    incoming = lax.all_to_all(
        outgoing.reshape(owner_count, slot_cap, width_local),
        ("req", "seq"),
        split_axis=0,
        concat_axis=0,
        tiled=True,
    )
    return incoming.reshape(1, owner_count, slot_cap, width_local)


def solution(mesh):
    return jax.shard_map(
        per_device,
        mesh=mesh,
        in_specs=(
            P("req", "seq", "tp"),
            P("req", "seq", None, "tp"),
            P("req", "seq", None, "tp"),
            P("req"),
            P("req", "seq", "tp"),
            P(),
            P(None, "tp"),
            P(None, "tp"),
            P("tp", None),
            P(("req", "seq"), None, None),
        ),
        out_specs=P(("req", "seq"), None, None, "tp"),
        check_vma=False,
    )
```

```python
import functools

import jax
import jax.numpy as jnp
from jax import lax
from jax.experimental import pallas as pl
from jax.experimental.pallas import tpu as pltpu
from jax.sharding import PartitionSpec as P

HEAD = 96

masked_floor = -1e30
LANE = 128


def attention_kernel(meta_ref, q_ref, kc_ref, vc_ref, kf_ref, vf_ref, sum_ref, stat_ref, *, tq, heads):
    slot = pl.program_id(0)
    q_block = pl.program_id(1)
    seq_index = meta_ref[0]
    length = meta_ref[1 + slot]
    span = kc_ref.shape[0]
    fresh_count = kf_ref.shape[0]
    width = q_ref.shape[-1]
    offset = seq_index * span
    scale = HEAD ** (-0.5)

    q = q_ref[...].reshape(tq, q_ref.shape[-1])
    lane = lax.broadcasted_iota(jnp.int32, (1, width), 1)
    stat_lane = lax.broadcasted_iota(jnp.int32, (1, 2 * heads), 1)
    rows = q_block * tq + lax.broadcasted_iota(jnp.int32, (tq, 1), 0)
    fresh_cols = seq_index * fresh_count + lax.broadcasted_iota(jnp.int32, (1, fresh_count), 1)
    fresh_visible = fresh_cols <= rows
    cached_visible = (offset + lax.broadcasted_iota(jnp.int32, (1, span), 1)) < length
    contract = (((1,), (1,)), ((), ()))

    def run(with_cache, masked=True):
        kf = kf_ref[...]
        vf = vf_ref[...]
        if with_cache:
            kc = kc_ref[...]
            vc = vc_ref[...]
        tiles = [jnp.zeros((tq, LANE), jnp.float32) for _ in range(width // LANE)]
        stats = jnp.zeros((tq, 2 * heads), jnp.float32)
        for h in range(heads):
            lo = h * HEAD // LANE * LANE
            hi = -(-(h + 1) * HEAD // LANE) * LANE
            head_lanes = (lane >= h * HEAD) & (lane < (h + 1) * HEAD)
            qh = jnp.where(head_lanes[:, lo:hi], q[:, lo:hi], jnp.zeros_like(q[:, lo:hi]))
            sf = lax.dot_general(qh, kf[:, lo:hi], contract, preferred_element_type=jnp.float32)
            sf = jnp.where(fresh_visible, sf, masked_floor)
            peak = jnp.max(sf, axis=-1, keepdims=True)
            if with_cache:
                sc = lax.dot_general(qh, kc[:, lo:hi], contract, preferred_element_type=jnp.float32)
                if masked:
                    sc = jnp.where(cached_visible, sc, masked_floor)
                peak = jnp.maximum(peak, jnp.max(sc, axis=-1, keepdims=True))
            pf = jnp.where(fresh_visible, jnp.exp((sf - peak) * scale), 0.0)
            total = jnp.sum(pf, axis=-1, keepdims=True)
            oh = jnp.dot(pf.astype(jnp.bfloat16), vf[:, lo:hi], preferred_element_type=jnp.float32)
            if with_cache:
                pc = jnp.exp((sc - peak) * scale)
                total = total + jnp.sum(pc, axis=-1, keepdims=True)
                oh = oh + jnp.dot(pc.astype(jnp.bfloat16), vc[:, lo:hi], preferred_element_type=jnp.float32)
            for j in range(lo // LANE, hi // LANE):
                part = oh[:, j * LANE - lo:(j + 1) * LANE - lo]
                tiles[j] = jnp.where(head_lanes[:, j * LANE:(j + 1) * LANE], part, tiles[j])
            stats = jnp.where(stat_lane == h, peak * scale, stats)
            stats = jnp.where(stat_lane == heads + h, total, stats)
        weighted = jnp.concatenate(tiles, axis=1)
        sum_ref[...] = weighted.reshape(sum_ref.shape).astype(sum_ref.dtype)
        stat_ref[...] = stats.reshape(stat_ref.shape)

    @pl.when((offset < length) & (offset + span > length))
    def _():
        run(True)

    @pl.when(offset + span <= length)
    def _():
        run(True, masked=False)

    @pl.when(offset >= length)
    def _():
        run(False)


def local_attention(all_queries, cache_kv, new_kv, cached_len, seq_index):
    source_count, slot_count, token_count, width = all_queries.shape
    query_count = source_count * token_count
    span = cache_kv.shape[1]
    fresh_count = new_kv.shape[1]
    heads = width // HEAD
    tq = 256 if query_count % 256 == 0 else query_count
    cache2 = cache_kv.reshape(slot_count, span, 2 * width)
    fresh2 = new_kv.reshape(slot_count, fresh_count, 2 * width)
    meta = jnp.concatenate([jnp.reshape(seq_index, (1,)).astype(jnp.int32), cached_len.astype(jnp.int32)])
    kernel = functools.partial(attention_kernel, tq=tq, heads=heads)
    grid_spec = pltpu.PrefetchScalarGridSpec(
        num_scalar_prefetch=1,
        grid=(slot_count, query_count // tq),
        in_specs=[
            pl.BlockSpec((tq // token_count, None, token_count, width), lambda s, b, m: (b, s, 0, 0)),
            pl.BlockSpec((None, span, width), lambda s, b, m: (s, 0, 0)),
            pl.BlockSpec((None, span, width), lambda s, b, m: (s, 0, 1)),
            pl.BlockSpec((None, fresh_count, width), lambda s, b, m: (s, 0, 0)),
            pl.BlockSpec((None, fresh_count, width), lambda s, b, m: (s, 0, 1)),
        ],
        out_specs=[
            pl.BlockSpec((tq // token_count, None, token_count, width), lambda s, b, m: (b, s, 0, 0)),
            pl.BlockSpec((tq // token_count, None, token_count, 2 * heads), lambda s, b, m: (b, s, 0, 0)),
        ],
    )
    return pl.pallas_call(
        kernel,
        grid_spec=grid_spec,
        out_shape=[
            jax.ShapeDtypeStruct((source_count, slot_count, token_count, width), jnp.bfloat16),
            jax.ShapeDtypeStruct((source_count, slot_count, token_count, 2 * heads), jnp.float32),
        ],
    )(meta, all_queries, cache2, cache2, fresh2, fresh2)


def combine_kernel(sum_ref, stat_ref, residual_ref, out_ref, *, heads):
    stats = stat_ref[...]
    sums = sum_ref[...].astype(jnp.float32)
    width = sums.shape[-1]
    lane = lax.broadcasted_iota(jnp.int32, (1, width), 1)
    attention = jnp.zeros(sums.shape[1:], jnp.float32)
    for h in range(heads):
        peak = stats[:, :, h:h + 1]
        joint_peak = jnp.max(peak, axis=0)
        scale = jnp.exp(peak - joint_peak[None])
        total = jnp.sum(stats[:, :, heads + h:heads + h + 1] * scale, axis=0)
        head_sum = jnp.sum(sums * scale, axis=0)
        head_lanes = (lane >= h * HEAD) & (lane < (h + 1) * HEAD)
        attention = jnp.where(head_lanes, head_sum / total, attention)
    out_ref[...] = (residual_ref[...].astype(jnp.float32) + attention).astype(out_ref.dtype)


def combine(source_sum, source_stats, residual_rows):
    heads = source_stats.shape[-1] // 2
    return pl.pallas_call(
        functools.partial(combine_kernel, heads=heads),
        out_shape=jax.ShapeDtypeStruct(residual_rows.shape, jnp.bfloat16),
    )(source_sum, source_stats, residual_rows)


def normalize(features, norm_gain):
    values = features.astype(jnp.float32)
    mean_square = jnp.mean(values * values, axis=-1, keepdims=True)
    return (values * lax.rsqrt(mean_square + 1e-05) * norm_gain).astype(jnp.bfloat16)


def per_device(
    queries, new_kv, cache_kv, cached_len, residual_in, norm_gain, gate_w, up_w, down_w, owner
):
    slot_count, token_count, width_local = queries.shape
    head_count = width_local // HEAD
    seq_index = lax.axis_index("seq")
    seq_count = lax.axis_size("seq")
    all_queries = lax.all_to_all(
        jnp.broadcast_to(queries[None], (seq_count,) + queries.shape), "seq", 0, 0, tiled=True
    )
    partial_sum, partial_stats = local_attention(all_queries, cache_kv, new_kv, cached_len, seq_index)
    source_sum = lax.all_to_all(partial_sum, "seq", 0, 0, tiled=True)
    source_stats = lax.all_to_all(partial_stats, "seq", 0, 0, tiled=True)
    row_count = slot_count * token_count
    block_rows = combine(
        source_sum.reshape(seq_count, row_count, width_local),
        source_stats.reshape(seq_count, row_count, 2 * head_count),
        residual_in.reshape(row_count, width_local),
    )
    tp_count = lax.axis_size("tp")
    full_rows = (
        lax.all_to_all(
            jnp.broadcast_to(block_rows[None], (tp_count,) + block_rows.shape), "tp", 0, 0, tiled=True
        )
        .transpose(1, 0, 2)
        .reshape(row_count, tp_count * width_local)
    )
    normed = normalize(full_rows, norm_gain)
    gate_out = jnp.dot(normed, gate_w, preferred_element_type=jnp.float32)
    up_out = jnp.dot(normed, up_w, preferred_element_type=jnp.float32)
    hidden = (jax.nn.silu(gate_out) * up_out).astype(jnp.bfloat16)
    partial_sum = jnp.dot(hidden, down_w, preferred_element_type=jnp.float32)
    pieces = partial_sum.astype(jnp.bfloat16).reshape(row_count, tp_count, width_local).transpose(1, 0, 2)
    unit_share = jnp.sum(
        lax.all_to_all(pieces, "tp", 0, 0, tiled=True).astype(jnp.float32), axis=0
    )
    finished = (block_rows.astype(jnp.float32) + unit_share).astype(jnp.bfloat16)

    owner_ids = owner.reshape(-1)
    owner_count = lax.axis_size(("req", "seq"))
    slot_cap = max(2, 2 * row_count // owner_count)
    matches = (owner_ids[:, None] == jnp.arange(owner_count, dtype=jnp.int32)[None, :]).astype(
        jnp.int32
    )
    ranking = jnp.sum(jnp.cumsum(matches, axis=0) * matches, axis=1) - 1
    outgoing = (
        jnp.zeros((owner_count * slot_cap, width_local), jnp.bfloat16)
        .at[owner_ids * slot_cap + ranking]
        .set(finished)
    )
    incoming = lax.all_to_all(
        outgoing.reshape(owner_count, slot_cap, width_local),
        ("req", "seq"),
        split_axis=0,
        concat_axis=0,
        tiled=True,
    )
    return incoming.reshape(1, owner_count, slot_cap, width_local)


def solution(mesh):
    return jax.shard_map(
        per_device,
        mesh=mesh,
        in_specs=(
            P("req", "seq", "tp"),
            P("req", "seq", None, "tp"),
            P("req", "seq", None, "tp"),
            P("req"),
            P("req", "seq", "tp"),
            P(),
            P(None, "tp"),
            P(None, "tp"),
            P("tp", None),
            P(("req", "seq"), None, None),
        ),
        out_specs=P(("req", "seq"), None, None, "tp"),
        check_vma=False,
    )
```

```python
import functools

import jax
import jax.numpy as jnp
from jax import lax
from jax.experimental import pallas as pl
from jax.experimental.pallas import tpu as pltpu
from jax.sharding import PartitionSpec as P

HEAD = 96

masked_floor = -1e30
LANE = 128


def attention_kernel(meta_ref, q_ref, kc_ref, vc_ref, kf_ref, vf_ref, sum_ref, stat_ref, *, tq, heads):
    slot = pl.program_id(0)
    q_block = pl.program_id(1)
    seq_index = meta_ref[0]
    length = meta_ref[1 + slot]
    span = kc_ref.shape[0]
    fresh_count = kf_ref.shape[0]
    width = q_ref.shape[-1]
    offset = seq_index * span
    scale = HEAD ** (-0.5)

    q = q_ref[...].reshape(tq, q_ref.shape[-1])
    lane = lax.broadcasted_iota(jnp.int32, (1, width), 1)
    stat_lane = lax.broadcasted_iota(jnp.int32, (1, 2 * heads), 1)
    rows = q_block * tq + lax.broadcasted_iota(jnp.int32, (tq, 1), 0)
    fresh_cols = seq_index * fresh_count + lax.broadcasted_iota(jnp.int32, (1, fresh_count), 1)
    fresh_visible = fresh_cols <= rows
    cached_visible = (offset + lax.broadcasted_iota(jnp.int32, (1, span), 1)) < length
    contract = (((1,), (1,)), ((), ()))

    def run(with_cache, masked=True):
        kf = kf_ref[...]
        vf = vf_ref[...]
        if with_cache:
            kc = kc_ref[...]
            vc = vc_ref[...]
        tiles = [jnp.zeros((tq, LANE), jnp.float32) for _ in range(width // LANE)]
        stats = jnp.zeros((tq, 2 * heads), jnp.float32)
        for h in range(heads):
            lo = h * HEAD // LANE * LANE
            hi = -(-(h + 1) * HEAD // LANE) * LANE
            head_lanes = (lane >= h * HEAD) & (lane < (h + 1) * HEAD)
            qh = jnp.where(head_lanes[:, lo:hi], q[:, lo:hi], jnp.zeros_like(q[:, lo:hi]))
            sf = lax.dot_general(qh, kf[:, lo:hi], contract, preferred_element_type=jnp.float32)
            sf = jnp.where(fresh_visible, sf, masked_floor)
            peak = jnp.max(sf, axis=-1, keepdims=True)
            if with_cache:
                sc = lax.dot_general(qh, kc[:, lo:hi], contract, preferred_element_type=jnp.float32)
                if masked:
                    sc = jnp.where(cached_visible, sc, masked_floor)
                peak = jnp.maximum(peak, jnp.max(sc, axis=-1, keepdims=True))
            pf = jnp.where(fresh_visible, jnp.exp((sf - peak) * scale), 0.0)
            total = jnp.sum(pf, axis=-1, keepdims=True)
            oh = jnp.dot(pf.astype(jnp.bfloat16), vf[:, lo:hi], preferred_element_type=jnp.float32)
            if with_cache:
                pc = jnp.exp((sc - peak) * scale)
                total = total + jnp.sum(pc, axis=-1, keepdims=True)
                oh = oh + jnp.dot(pc.astype(jnp.bfloat16), vc[:, lo:hi], preferred_element_type=jnp.float32)
            for j in range(lo // LANE, hi // LANE):
                part = oh[:, j * LANE - lo:(j + 1) * LANE - lo]
                tiles[j] = jnp.where(head_lanes[:, j * LANE:(j + 1) * LANE], part, tiles[j])
            stats = jnp.where(stat_lane == h, peak * scale, stats)
            stats = jnp.where(stat_lane == heads + h, total, stats)
        weighted = jnp.concatenate(tiles, axis=1)
        sum_ref[...] = weighted.reshape(sum_ref.shape).astype(sum_ref.dtype)
        stat_ref[...] = stats.reshape(stat_ref.shape)

    @pl.when((offset < length) & (offset + span > length))
    def _():
        run(True)

    @pl.when(offset + span <= length)
    def _():
        run(True, masked=False)

    @pl.when(offset >= length)
    def _():
        run(False)


def local_attention(all_queries, cache_kv, new_kv, cached_len, seq_index):
    source_count, slot_count, token_count, width = all_queries.shape
    query_count = source_count * token_count
    span = cache_kv.shape[1]
    fresh_count = new_kv.shape[1]
    heads = width // HEAD
    tq = query_count
    cache2 = cache_kv.transpose(0, 2, 1, 3)
    fresh2 = new_kv.transpose(0, 2, 1, 3)
    meta = jnp.concatenate([jnp.reshape(seq_index, (1,)).astype(jnp.int32), cached_len.astype(jnp.int32)])
    kernel = functools.partial(attention_kernel, tq=tq, heads=heads)
    grid_spec = pltpu.PrefetchScalarGridSpec(
        num_scalar_prefetch=1,
        grid=(slot_count, query_count // tq),
        in_specs=[
            pl.BlockSpec((tq // token_count, None, token_count, width), lambda s, b, m: (b, s, 0, 0)),
            pl.BlockSpec((None, None, span, width), lambda s, b, m: (s, 0, 0, 0)),
            pl.BlockSpec((None, None, span, width), lambda s, b, m: (s, 1, 0, 0)),
            pl.BlockSpec((None, None, fresh_count, width), lambda s, b, m: (s, 0, 0, 0)),
            pl.BlockSpec((None, None, fresh_count, width), lambda s, b, m: (s, 1, 0, 0)),
        ],
        out_specs=[
            pl.BlockSpec((tq // token_count, None, token_count, width), lambda s, b, m: (b, s, 0, 0)),
            pl.BlockSpec((tq // token_count, None, token_count, 2 * heads), lambda s, b, m: (b, s, 0, 0)),
        ],
    )
    return pl.pallas_call(
        kernel,
        grid_spec=grid_spec,
        out_shape=[
            jax.ShapeDtypeStruct((source_count, slot_count, token_count, width), jnp.bfloat16),
            jax.ShapeDtypeStruct((source_count, slot_count, token_count, 2 * heads), jnp.float32),
        ],
    )(meta, all_queries, cache2, cache2, fresh2, fresh2)


def combine_kernel(sum_ref, stat_ref, residual_ref, out_ref, *, heads):
    stats = stat_ref[...]
    sums = sum_ref[...].astype(jnp.float32)
    width = sums.shape[-1]
    lane = lax.broadcasted_iota(jnp.int32, (1, width), 1)
    attention = jnp.zeros(sums.shape[1:], jnp.float32)
    for h in range(heads):
        peak = stats[:, :, h:h + 1]
        joint_peak = jnp.max(peak, axis=0)
        scale = jnp.exp(peak - joint_peak[None])
        total = jnp.sum(stats[:, :, heads + h:heads + h + 1] * scale, axis=0)
        head_sum = jnp.sum(sums * scale, axis=0)
        head_lanes = (lane >= h * HEAD) & (lane < (h + 1) * HEAD)
        attention = jnp.where(head_lanes, head_sum / total, attention)
    out_ref[...] = (residual_ref[...].astype(jnp.float32) + attention).astype(out_ref.dtype)


def combine(source_sum, source_stats, residual_rows):
    heads = source_stats.shape[-1] // 2
    return pl.pallas_call(
        functools.partial(combine_kernel, heads=heads),
        out_shape=jax.ShapeDtypeStruct(residual_rows.shape, jnp.bfloat16),
    )(source_sum, source_stats, residual_rows)


def normalize(features, norm_gain):
    values = features.astype(jnp.float32)
    mean_square = jnp.mean(values * values, axis=-1, keepdims=True)
    return (values * lax.rsqrt(mean_square + 1e-05) * norm_gain).astype(jnp.bfloat16)


def per_device(
    queries, new_kv, cache_kv, cached_len, residual_in, norm_gain, gate_w, up_w, down_w, owner
):
    slot_count, token_count, width_local = queries.shape
    head_count = width_local // HEAD
    seq_index = lax.axis_index("seq")
    seq_count = lax.axis_size("seq")
    all_queries = lax.all_to_all(
        jnp.broadcast_to(queries[None], (seq_count,) + queries.shape), "seq", 0, 0, tiled=True
    )
    partial_sum, partial_stats = local_attention(all_queries, cache_kv, new_kv, cached_len, seq_index)
    source_sum = lax.all_to_all(partial_sum, "seq", 0, 0, tiled=True)
    source_stats = lax.all_to_all(partial_stats, "seq", 0, 0, tiled=True)
    row_count = slot_count * token_count
    block_rows = combine(
        source_sum.reshape(seq_count, row_count, width_local),
        source_stats.reshape(seq_count, row_count, 2 * head_count),
        residual_in.reshape(row_count, width_local),
    )
    tp_count = lax.axis_size("tp")
    full_rows = (
        lax.all_to_all(
            jnp.broadcast_to(block_rows[None], (tp_count,) + block_rows.shape), "tp", 0, 0, tiled=True
        )
        .transpose(1, 0, 2)
        .reshape(row_count, tp_count * width_local)
    )
    normed = normalize(full_rows, norm_gain)
    gate_out = jnp.dot(normed, gate_w, preferred_element_type=jnp.float32)
    up_out = jnp.dot(normed, up_w, preferred_element_type=jnp.float32)
    hidden = (jax.nn.silu(gate_out) * up_out).astype(jnp.bfloat16)
    partial_sum = jnp.dot(hidden, down_w, preferred_element_type=jnp.float32)
    pieces = partial_sum.astype(jnp.bfloat16).reshape(row_count, tp_count, width_local).transpose(1, 0, 2)
    unit_share = jnp.sum(
        lax.all_to_all(pieces, "tp", 0, 0, tiled=True).astype(jnp.float32), axis=0
    )
    finished = (block_rows.astype(jnp.float32) + unit_share).astype(jnp.bfloat16)

    owner_ids = owner.reshape(-1)
    owner_count = lax.axis_size(("req", "seq"))
    slot_cap = max(2, 2 * row_count // owner_count)
    matches = (owner_ids[:, None] == jnp.arange(owner_count, dtype=jnp.int32)[None, :]).astype(
        jnp.int32
    )
    ranking = jnp.sum(jnp.cumsum(matches, axis=0) * matches, axis=1) - 1
    outgoing = (
        jnp.zeros((owner_count * slot_cap, width_local), jnp.bfloat16)
        .at[owner_ids * slot_cap + ranking]
        .set(finished)
    )
    incoming = lax.all_to_all(
        outgoing.reshape(owner_count, slot_cap, width_local),
        ("req", "seq"),
        split_axis=0,
        concat_axis=0,
        tiled=True,
    )
    return incoming.reshape(1, owner_count, slot_cap, width_local)


def solution(mesh):
    return jax.shard_map(
        per_device,
        mesh=mesh,
        in_specs=(
            P("req", "seq", "tp"),
            P("req", "seq", None, "tp"),
            P("req", "seq", None, "tp"),
            P("req"),
            P("req", "seq", "tp"),
            P(),
            P(None, "tp"),
            P(None, "tp"),
            P("tp", None),
            P(("req", "seq"), None, None),
        ),
        out_specs=P(("req", "seq"), None, None, "tp"),
        check_vma=False,
    )
```

```python
import functools

import jax
import jax.numpy as jnp
from jax import lax
from jax.experimental import pallas as pl
from jax.experimental.pallas import tpu as pltpu
from jax.sharding import PartitionSpec as P

HEAD = 96

masked_floor = -1e30
LANE = 128


def attention_kernel(meta_ref, q_ref, kc_ref, vc_ref, kf_ref, vf_ref, sum_ref, stat_ref, *, tq, heads):
    slot = pl.program_id(0)
    q_block = pl.program_id(1)
    seq_index = meta_ref[0]
    length = meta_ref[1 + slot]
    span = kc_ref.shape[0]
    fresh_count = kf_ref.shape[0]
    width = q_ref.shape[-1]
    offset = seq_index * span
    scale = HEAD ** (-0.5)

    q = q_ref[...].reshape(tq, q_ref.shape[-1])
    lane = lax.broadcasted_iota(jnp.int32, (1, width), 1)
    stat_lane = lax.broadcasted_iota(jnp.int32, (1, 2 * heads), 1)
    rows = q_block * tq + lax.broadcasted_iota(jnp.int32, (tq, 1), 0)
    fresh_cols = seq_index * fresh_count + lax.broadcasted_iota(jnp.int32, (1, fresh_count), 1)
    fresh_visible = fresh_cols <= rows
    cached_visible = (offset + lax.broadcasted_iota(jnp.int32, (1, span), 1)) < length
    contract = (((1,), (1,)), ((), ()))

    def run(with_cache, masked=True):
        kf = kf_ref[...]
        vf = vf_ref[...]
        if with_cache:
            kc = kc_ref[...]
            vc = vc_ref[...]
        tiles = [jnp.zeros((tq, LANE), jnp.float32) for _ in range(width // LANE)]
        stats = jnp.zeros((tq, 2 * heads), jnp.float32)
        for h in range(heads):
            lo = h * HEAD // LANE * LANE
            hi = -(-(h + 1) * HEAD // LANE) * LANE
            head_lanes = (lane >= h * HEAD) & (lane < (h + 1) * HEAD)
            qh = jnp.where(head_lanes[:, lo:hi], q[:, lo:hi], jnp.zeros_like(q[:, lo:hi]))
            sf = lax.dot_general(qh, kf[:, lo:hi], contract, preferred_element_type=jnp.float32)
            sf = jnp.where(fresh_visible, sf, masked_floor)
            peak = jnp.max(sf, axis=-1, keepdims=True)
            if with_cache:
                sc = lax.dot_general(qh, kc[:, lo:hi], contract, preferred_element_type=jnp.float32)
                if masked:
                    sc = jnp.where(cached_visible, sc, masked_floor)
                peak = jnp.maximum(peak, jnp.max(sc, axis=-1, keepdims=True))
            pf = jnp.where(fresh_visible, jnp.exp((sf - peak) * scale), 0.0)
            total = jnp.sum(pf, axis=-1, keepdims=True)
            oh = jnp.dot(pf.astype(jnp.bfloat16), vf[:, lo:hi], preferred_element_type=jnp.float32)
            if with_cache:
                pc = jnp.exp((sc - peak) * scale)
                total = total + jnp.sum(pc, axis=-1, keepdims=True)
                oh = oh + jnp.dot(pc.astype(jnp.bfloat16), vc[:, lo:hi], preferred_element_type=jnp.float32)
            for j in range(lo // LANE, hi // LANE):
                part = oh[:, j * LANE - lo:(j + 1) * LANE - lo]
                tiles[j] = jnp.where(head_lanes[:, j * LANE:(j + 1) * LANE], part, tiles[j])
            stats = jnp.where(stat_lane == h, peak * scale, stats)
            stats = jnp.where(stat_lane == heads + h, total, stats)
        weighted = jnp.concatenate(tiles, axis=1)
        sum_ref[...] = weighted.reshape(sum_ref.shape).astype(sum_ref.dtype)
        stat_ref[...] = stats.reshape(stat_ref.shape)

    @pl.when((offset < length) & (offset + span > length))
    def _():
        run(True)

    @pl.when(offset + span <= length)
    def _():
        run(True, masked=False)

    @pl.when(offset >= length)
    def _():
        run(False)


def local_attention(all_queries, cache_kv, new_kv, cached_len, seq_index):
    source_count, slot_count, token_count, width = all_queries.shape
    query_count = source_count * token_count
    span = cache_kv.shape[1]
    fresh_count = new_kv.shape[1]
    heads = width // HEAD
    tq = query_count
    cache2 = cache_kv.transpose(0, 2, 1, 3)
    fresh2 = new_kv.transpose(0, 2, 1, 3)
    meta = jnp.concatenate([jnp.reshape(seq_index, (1,)).astype(jnp.int32), cached_len.astype(jnp.int32)])
    kernel = functools.partial(attention_kernel, tq=tq, heads=heads)
    grid_spec = pltpu.PrefetchScalarGridSpec(
        num_scalar_prefetch=1,
        grid=(slot_count, query_count // tq),
        in_specs=[
            pl.BlockSpec((tq // token_count, None, token_count, width), lambda s, b, m: (b, s, 0, 0)),
            pl.BlockSpec((None, None, span, width), lambda s, b, m: (s, 0, 0, 0)),
            pl.BlockSpec((None, None, span, width), lambda s, b, m: (s, 1, 0, 0)),
            pl.BlockSpec((None, None, fresh_count, width), lambda s, b, m: (s, 0, 0, 0)),
            pl.BlockSpec((None, None, fresh_count, width), lambda s, b, m: (s, 1, 0, 0)),
        ],
        out_specs=[
            pl.BlockSpec((tq // token_count, None, token_count, width), lambda s, b, m: (b, s, 0, 0)),
            pl.BlockSpec((tq // token_count, None, token_count, 2 * heads), lambda s, b, m: (b, s, 0, 0)),
        ],
    )
    return pl.pallas_call(
        kernel,
        grid_spec=grid_spec,
        out_shape=[
            jax.ShapeDtypeStruct((source_count, slot_count, token_count, width), jnp.bfloat16),
            jax.ShapeDtypeStruct((source_count, slot_count, token_count, 2 * heads), jnp.float32),
        ],
    )(meta, all_queries, cache2, cache2, fresh2, fresh2)


def combine_kernel(sum_ref, stat_ref, residual_ref, out_ref, copies_ref, *, heads):
    stats = stat_ref[...]
    width = sum_ref.shape[-1]
    lane = lax.broadcasted_iota(jnp.int32, (1, width), 1)
    tiles = [jnp.zeros((sum_ref.shape[1], LANE), jnp.float32) for _ in range(width // LANE)]
    for h in range(heads):
        lo = h * HEAD // LANE * LANE
        hi = -(-(h + 1) * HEAD // LANE) * LANE
        peak = stats[:, :, h:h + 1]
        joint_peak = jnp.max(peak, axis=0)
        scale = jnp.exp(peak - joint_peak[None])
        total = jnp.sum(stats[:, :, heads + h:heads + h + 1] * scale, axis=0)
        head_sum = jnp.sum(sum_ref[:, :, lo:hi].astype(jnp.float32) * scale, axis=0)
        value = head_sum / total
        for j in range(lo // LANE, hi // LANE):
            head_lanes = (lane[:, j * LANE:(j + 1) * LANE] >= h * HEAD) & (
                lane[:, j * LANE:(j + 1) * LANE] < (h + 1) * HEAD
            )
            tiles[j] = jnp.where(head_lanes, value[:, j * LANE - lo:(j + 1) * LANE - lo], tiles[j])
    attention = jnp.concatenate(tiles, axis=1)
    rows = (residual_ref[...].astype(jnp.float32) + attention).astype(out_ref.dtype)
    out_ref[...] = rows
    for k in range(copies_ref.shape[0]):
        copies_ref[k] = rows


def combine(source_sum, source_stats, residual_rows, copies):
    heads = source_stats.shape[-1] // 2
    return pl.pallas_call(
        functools.partial(combine_kernel, heads=heads),
        out_shape=[
            jax.ShapeDtypeStruct(residual_rows.shape, jnp.bfloat16),
            jax.ShapeDtypeStruct((copies,) + residual_rows.shape, jnp.bfloat16),
        ],
    )(source_sum, source_stats, residual_rows)


def normalize(features, norm_gain):
    values = features.astype(jnp.float32)
    mean_square = jnp.mean(values * values, axis=-1, keepdims=True)
    return (values * lax.rsqrt(mean_square + 1e-05) * norm_gain).astype(jnp.bfloat16)


def per_device(
    queries, new_kv, cache_kv, cached_len, residual_in, norm_gain, gate_w, up_w, down_w, owner
):
    slot_count, token_count, width_local = queries.shape
    head_count = width_local // HEAD
    seq_index = lax.axis_index("seq")
    seq_count = lax.axis_size("seq")
    all_queries = lax.all_to_all(
        jnp.broadcast_to(queries[None], (seq_count,) + queries.shape), "seq", 0, 0, tiled=True
    )
    partial_sum, partial_stats = local_attention(all_queries, cache_kv, new_kv, cached_len, seq_index)
    source_sum = lax.all_to_all(partial_sum, "seq", 0, 0, tiled=True)
    source_stats = lax.all_to_all(partial_stats, "seq", 0, 0, tiled=True)
    row_count = slot_count * token_count
    tp_count = lax.axis_size("tp")
    block_rows, row_copies = combine(
        source_sum.reshape(seq_count, row_count, width_local),
        source_stats.reshape(seq_count, row_count, 2 * head_count),
        residual_in.reshape(row_count, width_local),
        tp_count,
    )
    full_rows = (
        lax.all_to_all(
            row_copies, "tp", 0, 0, tiled=True
        )
        .transpose(1, 0, 2)
        .reshape(row_count, tp_count * width_local)
    )
    normed = normalize(full_rows, norm_gain)
    gate_out = jnp.dot(normed, gate_w, preferred_element_type=jnp.float32)
    up_out = jnp.dot(normed, up_w, preferred_element_type=jnp.float32)
    hidden = (jax.nn.silu(gate_out) * up_out).astype(jnp.bfloat16)
    partial_sum = jnp.dot(hidden, down_w, preferred_element_type=jnp.float32)
    pieces = partial_sum.astype(jnp.bfloat16).reshape(row_count, tp_count, width_local).transpose(1, 0, 2)
    unit_share = jnp.sum(
        lax.all_to_all(pieces, "tp", 0, 0, tiled=True).astype(jnp.float32), axis=0
    )
    finished = (block_rows.astype(jnp.float32) + unit_share).astype(jnp.bfloat16)

    owner_ids = owner.reshape(-1)
    owner_count = lax.axis_size(("req", "seq"))
    slot_cap = max(2, 2 * row_count // owner_count)
    matches = (owner_ids[:, None] == jnp.arange(owner_count, dtype=jnp.int32)[None, :]).astype(
        jnp.int32
    )
    ranking = jnp.sum(jnp.cumsum(matches, axis=0) * matches, axis=1) - 1
    outgoing = (
        jnp.zeros((owner_count * slot_cap, width_local), jnp.bfloat16)
        .at[owner_ids * slot_cap + ranking]
        .set(finished)
    )
    incoming = lax.all_to_all(
        outgoing.reshape(owner_count, slot_cap, width_local),
        ("req", "seq"),
        split_axis=0,
        concat_axis=0,
        tiled=True,
    )
    return incoming.reshape(1, owner_count, slot_cap, width_local)


def solution(mesh):
    return jax.shard_map(
        per_device,
        mesh=mesh,
        in_specs=(
            P("req", "seq", "tp"),
            P("req", "seq", None, "tp"),
            P("req", "seq", None, "tp"),
            P("req"),
            P("req", "seq", "tp"),
            P(),
            P(None, "tp"),
            P(None, "tp"),
            P("tp", None),
            P(("req", "seq"), None, None),
        ),
        out_specs=P(("req", "seq"), None, None, "tp"),
        check_vma=False,
    )
```

```python
import functools

import jax
import jax.numpy as jnp
from jax import lax
from jax.experimental import pallas as pl
from jax.experimental.pallas import tpu as pltpu
from jax.sharding import PartitionSpec as P

HEAD = 96

masked_floor = -1e30
LANE = 128
KEY_BLOCK = 256


def attention_kernel(meta_ref, q_ref, kc_ref, vc_ref, kf_ref, vf_ref, sum_ref, stat_ref, *, tq, heads):
    slot = pl.program_id(0)
    q_block = pl.program_id(1)
    seq_index = meta_ref[0]
    length = meta_ref[1 + slot]
    span = kc_ref.shape[0]
    fresh_count = kf_ref.shape[0]
    width = q_ref.shape[-1]
    offset = seq_index * span
    scale = HEAD ** (-0.5)

    q = q_ref[...].reshape(tq, q_ref.shape[-1])
    lane = lax.broadcasted_iota(jnp.int32, (1, width), 1)
    stat_lane = lax.broadcasted_iota(jnp.int32, (1, 2 * heads), 1)
    rows = q_block * tq + lax.broadcasted_iota(jnp.int32, (tq, 1), 0)
    fresh_cols = seq_index * fresh_count + lax.broadcasted_iota(jnp.int32, (1, fresh_count), 1)
    fresh_visible = fresh_cols <= rows
    cached_visible = (offset + lax.broadcasted_iota(jnp.int32, (1, span), 1)) < length
    contract = (((1,), (1,)), ((), ()))

    def run(with_cache, masked=True, keys=span):
        kf = kf_ref[...]
        vf = vf_ref[...]
        if with_cache:
            kc = kc_ref[:keys, :]
            vc = vc_ref[:keys, :]
            visible = cached_visible[:, :keys]
        tiles = [jnp.zeros((tq, LANE), jnp.float32) for _ in range(width // LANE)]
        stats = jnp.zeros((tq, 2 * heads), jnp.float32)
        for h in range(heads):
            lo = h * HEAD // LANE * LANE
            hi = -(-(h + 1) * HEAD // LANE) * LANE
            head_lanes = (lane >= h * HEAD) & (lane < (h + 1) * HEAD)
            qh = jnp.where(head_lanes[:, lo:hi], q[:, lo:hi], jnp.zeros_like(q[:, lo:hi]))
            sf = lax.dot_general(qh, kf[:, lo:hi], contract, preferred_element_type=jnp.float32)
            sf = jnp.where(fresh_visible, sf, masked_floor)
            peak = jnp.max(sf, axis=-1, keepdims=True)
            if with_cache:
                sc = lax.dot_general(qh, kc[:, lo:hi], contract, preferred_element_type=jnp.float32)
                if masked:
                    sc = jnp.where(visible, sc, masked_floor)
                peak = jnp.maximum(peak, jnp.max(sc, axis=-1, keepdims=True))
            pf = jnp.where(fresh_visible, jnp.exp((sf - peak) * scale), 0.0)
            total = jnp.sum(pf, axis=-1, keepdims=True)
            oh = jnp.dot(pf.astype(jnp.bfloat16), vf[:, lo:hi], preferred_element_type=jnp.float32)
            if with_cache:
                pc = jnp.exp((sc - peak) * scale)
                total = total + jnp.sum(pc, axis=-1, keepdims=True)
                oh = oh + jnp.dot(pc.astype(jnp.bfloat16), vc[:, lo:hi], preferred_element_type=jnp.float32)
            for j in range(lo // LANE, hi // LANE):
                part = oh[:, j * LANE - lo:(j + 1) * LANE - lo]
                tiles[j] = jnp.where(head_lanes[:, j * LANE:(j + 1) * LANE], part, tiles[j])
            stats = jnp.where(stat_lane == h, peak * scale, stats)
            stats = jnp.where(stat_lane == heads + h, total, stats)
        weighted = jnp.concatenate(tiles, axis=1)
        sum_ref[...] = weighted.reshape(sum_ref.shape).astype(sum_ref.dtype)
        stat_ref[...] = stats.reshape(stat_ref.shape)

    partial = (offset < length) & (offset + span > length)
    key_blocks = span // KEY_BLOCK
    used_blocks = (length - offset + KEY_BLOCK - 1) // KEY_BLOCK
    for used in range(1, key_blocks + 1):

        @pl.when(partial & (used_blocks == used))
        def _():
            run(True, keys=used * KEY_BLOCK)

    @pl.when(offset + span <= length)
    def _():
        run(True, masked=False)

    @pl.when(offset >= length)
    def _():
        run(False)


def local_attention(all_queries, cache_kv, new_kv, cached_len, seq_index):
    source_count, slot_count, token_count, width = all_queries.shape
    query_count = source_count * token_count
    span = cache_kv.shape[1]
    fresh_count = new_kv.shape[1]
    heads = width // HEAD
    tq = query_count
    cache2 = cache_kv.transpose(0, 2, 1, 3)
    fresh2 = new_kv.transpose(0, 2, 1, 3)
    meta = jnp.concatenate([jnp.reshape(seq_index, (1,)).astype(jnp.int32), cached_len.astype(jnp.int32)])
    kernel = functools.partial(attention_kernel, tq=tq, heads=heads)
    grid_spec = pltpu.PrefetchScalarGridSpec(
        num_scalar_prefetch=1,
        grid=(slot_count, query_count // tq),
        in_specs=[
            pl.BlockSpec((tq // token_count, None, token_count, width), lambda s, b, m: (b, s, 0, 0)),
            pl.BlockSpec((None, None, span, width), lambda s, b, m: (s, 0, 0, 0)),
            pl.BlockSpec((None, None, span, width), lambda s, b, m: (s, 1, 0, 0)),
            pl.BlockSpec((None, None, fresh_count, width), lambda s, b, m: (s, 0, 0, 0)),
            pl.BlockSpec((None, None, fresh_count, width), lambda s, b, m: (s, 1, 0, 0)),
        ],
        out_specs=[
            pl.BlockSpec((tq // token_count, None, token_count, width), lambda s, b, m: (b, s, 0, 0)),
            pl.BlockSpec((tq // token_count, None, token_count, 2 * heads), lambda s, b, m: (b, s, 0, 0)),
        ],
    )
    return pl.pallas_call(
        kernel,
        grid_spec=grid_spec,
        out_shape=[
            jax.ShapeDtypeStruct((source_count, slot_count, token_count, width), jnp.bfloat16),
            jax.ShapeDtypeStruct((source_count, slot_count, token_count, 2 * heads), jnp.float32),
        ],
    )(meta, all_queries, cache2, cache2, fresh2, fresh2)


def combine_kernel(sum_ref, stat_ref, residual_ref, out_ref, copies_ref, *, heads):
    stats = stat_ref[...]
    width = sum_ref.shape[-1]
    lane = lax.broadcasted_iota(jnp.int32, (1, width), 1)
    tiles = [jnp.zeros((sum_ref.shape[1], LANE), jnp.float32) for _ in range(width // LANE)]
    for h in range(heads):
        lo = h * HEAD // LANE * LANE
        hi = -(-(h + 1) * HEAD // LANE) * LANE
        peak = stats[:, :, h:h + 1]
        joint_peak = jnp.max(peak, axis=0)
        scale = jnp.exp(peak - joint_peak[None])
        total = jnp.sum(stats[:, :, heads + h:heads + h + 1] * scale, axis=0)
        head_sum = jnp.sum(sum_ref[:, :, lo:hi].astype(jnp.float32) * scale, axis=0)
        value = head_sum / total
        for j in range(lo // LANE, hi // LANE):
            head_lanes = (lane[:, j * LANE:(j + 1) * LANE] >= h * HEAD) & (
                lane[:, j * LANE:(j + 1) * LANE] < (h + 1) * HEAD
            )
            tiles[j] = jnp.where(head_lanes, value[:, j * LANE - lo:(j + 1) * LANE - lo], tiles[j])
    attention = jnp.concatenate(tiles, axis=1)
    rows = (residual_ref[...].astype(jnp.float32) + attention).astype(out_ref.dtype)
    out_ref[...] = rows
    for k in range(copies_ref.shape[0]):
        copies_ref[k] = rows


def combine(source_sum, source_stats, residual_rows, copies):
    heads = source_stats.shape[-1] // 2
    return pl.pallas_call(
        functools.partial(combine_kernel, heads=heads),
        out_shape=[
            jax.ShapeDtypeStruct(residual_rows.shape, jnp.bfloat16),
            jax.ShapeDtypeStruct((copies,) + residual_rows.shape, jnp.bfloat16),
        ],
    )(source_sum, source_stats, residual_rows)


def normalize(features, norm_gain):
    values = features.astype(jnp.float32)
    mean_square = jnp.mean(values * values, axis=-1, keepdims=True)
    return (values * lax.rsqrt(mean_square + 1e-05) * norm_gain).astype(jnp.bfloat16)


def per_device(
    queries, new_kv, cache_kv, cached_len, residual_in, norm_gain, gate_w, up_w, down_w, owner
):
    slot_count, token_count, width_local = queries.shape
    head_count = width_local // HEAD
    seq_index = lax.axis_index("seq")
    seq_count = lax.axis_size("seq")
    all_queries = lax.all_to_all(
        jnp.broadcast_to(queries[None], (seq_count,) + queries.shape), "seq", 0, 0, tiled=True
    )
    partial_sum, partial_stats = local_attention(all_queries, cache_kv, new_kv, cached_len, seq_index)
    source_sum = lax.all_to_all(partial_sum, "seq", 0, 0, tiled=True)
    source_stats = lax.all_to_all(partial_stats, "seq", 0, 0, tiled=True)
    row_count = slot_count * token_count
    tp_count = lax.axis_size("tp")
    block_rows, row_copies = combine(
        source_sum.reshape(seq_count, row_count, width_local),
        source_stats.reshape(seq_count, row_count, 2 * head_count),
        residual_in.reshape(row_count, width_local),
        tp_count,
    )
    full_rows = (
        lax.all_to_all(
            row_copies, "tp", 0, 0, tiled=True
        )
        .transpose(1, 0, 2)
        .reshape(row_count, tp_count * width_local)
    )
    normed = normalize(full_rows, norm_gain)
    gate_out = jnp.dot(normed, gate_w, preferred_element_type=jnp.float32)
    up_out = jnp.dot(normed, up_w, preferred_element_type=jnp.float32)
    hidden = (jax.nn.silu(gate_out) * up_out).astype(jnp.bfloat16)
    partial_sum = jnp.dot(hidden, down_w, preferred_element_type=jnp.float32)
    pieces = partial_sum.astype(jnp.bfloat16).reshape(row_count, tp_count, width_local).transpose(1, 0, 2)
    unit_share = jnp.sum(
        lax.all_to_all(pieces, "tp", 0, 0, tiled=True).astype(jnp.float32), axis=0
    )
    finished = (block_rows.astype(jnp.float32) + unit_share).astype(jnp.bfloat16)

    owner_ids = owner.reshape(-1)
    owner_count = lax.axis_size(("req", "seq"))
    slot_cap = max(2, 2 * row_count // owner_count)
    matches = (owner_ids[:, None] == jnp.arange(owner_count, dtype=jnp.int32)[None, :]).astype(
        jnp.int32
    )
    ranking = jnp.sum(jnp.cumsum(matches, axis=0) * matches, axis=1) - 1
    outgoing = (
        jnp.zeros((owner_count * slot_cap, width_local), jnp.bfloat16)
        .at[owner_ids * slot_cap + ranking]
        .set(finished)
    )
    incoming = lax.all_to_all(
        outgoing.reshape(owner_count, slot_cap, width_local),
        ("req", "seq"),
        split_axis=0,
        concat_axis=0,
        tiled=True,
    )
    return incoming.reshape(1, owner_count, slot_cap, width_local)


def solution(mesh):
    return jax.shard_map(
        per_device,
        mesh=mesh,
        in_specs=(
            P("req", "seq", "tp"),
            P("req", "seq", None, "tp"),
            P("req", "seq", None, "tp"),
            P("req"),
            P("req", "seq", "tp"),
            P(),
            P(None, "tp"),
            P(None, "tp"),
            P("tp", None),
            P(("req", "seq"), None, None),
        ),
        out_specs=P(("req", "seq"), None, None, "tp"),
        check_vma=False,
    )
```

```python
import functools

import jax
import jax.numpy as jnp
from jax import lax
from jax.experimental import pallas as pl
from jax.experimental.pallas import tpu as pltpu
from jax.sharding import PartitionSpec as P

HEAD = 96

masked_floor = -1e30
LANE = 128
KEY_BLOCK = 256


def attention_kernel(meta_ref, q_ref, kc_ref, vc_ref, kf_ref, vf_ref, sum_ref, stat_ref, *, tq, heads):
    slot = pl.program_id(0)
    q_block = pl.program_id(1)
    seq_index = meta_ref[0]
    length = meta_ref[1 + slot]
    span = kc_ref.shape[0]
    fresh_count = kf_ref.shape[0]
    width = q_ref.shape[-1]
    offset = seq_index * span
    scale = HEAD ** (-0.5)

    q = q_ref[...].reshape(tq, q_ref.shape[-1])
    lane = lax.broadcasted_iota(jnp.int32, (1, width), 1)
    stat_lane = lax.broadcasted_iota(jnp.int32, (1, 2 * heads), 1)
    rows = q_block * tq + lax.broadcasted_iota(jnp.int32, (tq, 1), 0)
    fresh_cols = seq_index * fresh_count + lax.broadcasted_iota(jnp.int32, (1, fresh_count), 1)
    fresh_visible = fresh_cols <= rows
    cached_visible = (offset + lax.broadcasted_iota(jnp.int32, (1, span), 1)) < length
    contract = (((1,), (1,)), ((), ()))

    def run(with_cache, masked=True, keys=span):
        kf = kf_ref[...]
        vf = vf_ref[...]
        if with_cache:
            kc = kc_ref[:keys, :]
            vc = vc_ref[:keys, :]
            visible = cached_visible[:, :keys]
        tiles = [jnp.zeros((tq, LANE), jnp.float32) for _ in range(width // LANE)]
        stats = jnp.zeros((tq, 2 * heads), jnp.float32)
        for h in range(heads):
            lo = h * HEAD // LANE * LANE
            hi = -(-(h + 1) * HEAD // LANE) * LANE
            head_lanes = (lane >= h * HEAD) & (lane < (h + 1) * HEAD)
            qh = jnp.where(head_lanes[:, lo:hi], q[:, lo:hi], jnp.zeros_like(q[:, lo:hi]))
            sf = lax.dot_general(qh, kf[:, lo:hi], contract, preferred_element_type=jnp.float32)
            sf = jnp.where(fresh_visible, sf, masked_floor)
            peak = jnp.max(sf, axis=-1, keepdims=True)
            if with_cache:
                sc = lax.dot_general(qh, kc[:, lo:hi], contract, preferred_element_type=jnp.float32)
                if masked:
                    sc = jnp.where(visible, sc, masked_floor)
                peak = jnp.maximum(peak, jnp.max(sc, axis=-1, keepdims=True))
            pf = jnp.where(fresh_visible, jnp.exp((sf - peak) * scale), 0.0)
            total = jnp.sum(pf, axis=-1, keepdims=True)
            oh = jnp.dot(pf.astype(jnp.bfloat16), vf[:, lo:hi], preferred_element_type=jnp.float32)
            if with_cache:
                pc = jnp.exp((sc - peak) * scale)
                total = total + jnp.sum(pc, axis=-1, keepdims=True)
                oh = oh + jnp.dot(pc.astype(jnp.bfloat16), vc[:, lo:hi], preferred_element_type=jnp.float32)
            for j in range(lo // LANE, hi // LANE):
                part = oh[:, j * LANE - lo:(j + 1) * LANE - lo]
                tiles[j] = jnp.where(head_lanes[:, j * LANE:(j + 1) * LANE], part, tiles[j])
            stats = jnp.where(stat_lane == h, peak * scale, stats)
            stats = jnp.where(stat_lane == heads + h, total, stats)
        weighted = jnp.concatenate(tiles, axis=1)
        sum_ref[...] = weighted.reshape(sum_ref.shape).astype(sum_ref.dtype)
        stat_ref[...] = stats.reshape(stat_ref.shape)

    partial = (offset < length) & (offset + span > length)
    key_blocks = span // KEY_BLOCK
    used_blocks = (length - offset + KEY_BLOCK - 1) // KEY_BLOCK
    for used in range(1, key_blocks + 1):

        @pl.when(partial & (used_blocks == used))
        def _():
            run(True, keys=used * KEY_BLOCK)

    @pl.when(offset + span <= length)
    def _():
        run(True, masked=False)

    @pl.when(offset >= length)
    def _():
        run(False)


def local_attention(all_queries, cache_kv, new_kv, cached_len, seq_index):
    source_count, slot_count, token_count, width = all_queries.shape
    query_count = source_count * token_count
    span = cache_kv.shape[1]
    fresh_count = new_kv.shape[1]
    heads = width // HEAD
    tq = query_count
    cache2 = cache_kv.transpose(0, 2, 1, 3)
    fresh2 = new_kv.transpose(0, 2, 1, 3)
    meta = jnp.concatenate([jnp.reshape(seq_index, (1,)).astype(jnp.int32), cached_len.astype(jnp.int32)])
    kernel = functools.partial(attention_kernel, tq=tq, heads=heads)
    grid_spec = pltpu.PrefetchScalarGridSpec(
        num_scalar_prefetch=1,
        grid=(slot_count, query_count // tq),
        in_specs=[
            pl.BlockSpec((tq // token_count, None, token_count, width), lambda s, b, m: (b, s, 0, 0)),
            pl.BlockSpec((None, None, span, width), lambda s, b, m: (s, 0, 0, 0)),
            pl.BlockSpec((None, None, span, width), lambda s, b, m: (s, 1, 0, 0)),
            pl.BlockSpec((None, None, fresh_count, width), lambda s, b, m: (s, 0, 0, 0)),
            pl.BlockSpec((None, None, fresh_count, width), lambda s, b, m: (s, 1, 0, 0)),
        ],
        out_specs=[
            pl.BlockSpec((tq // token_count, None, token_count, width), lambda s, b, m: (b, s, 0, 0)),
            pl.BlockSpec((tq // token_count, None, token_count, 2 * heads), lambda s, b, m: (b, s, 0, 0)),
        ],
    )
    return pl.pallas_call(
        kernel,
        grid_spec=grid_spec,
        out_shape=[
            jax.ShapeDtypeStruct((source_count, slot_count, token_count, width), jnp.bfloat16),
            jax.ShapeDtypeStruct((source_count, slot_count, token_count, 2 * heads), jnp.float32),
        ],
    )(meta, all_queries, cache2, cache2, fresh2, fresh2)


def combine_kernel(sum_ref, stat_ref, residual_ref, out_ref, copies_ref, *, heads):
    stats = stat_ref[...]
    width = sum_ref.shape[-1]
    lane = lax.broadcasted_iota(jnp.int32, (1, width), 1)
    tiles = [jnp.zeros((sum_ref.shape[1], LANE), jnp.float32) for _ in range(width // LANE)]
    for h in range(heads):
        lo = h * HEAD // LANE * LANE
        hi = -(-(h + 1) * HEAD // LANE) * LANE
        peak = stats[:, :, h:h + 1]
        joint_peak = jnp.max(peak, axis=0)
        scale = jnp.exp(peak - joint_peak[None])
        total = jnp.sum(stats[:, :, heads + h:heads + h + 1] * scale, axis=0)
        head_sum = jnp.sum(sum_ref[:, :, lo:hi].astype(jnp.float32) * scale, axis=0)
        value = head_sum / total
        for j in range(lo // LANE, hi // LANE):
            head_lanes = (lane[:, j * LANE:(j + 1) * LANE] >= h * HEAD) & (
                lane[:, j * LANE:(j + 1) * LANE] < (h + 1) * HEAD
            )
            tiles[j] = jnp.where(head_lanes, value[:, j * LANE - lo:(j + 1) * LANE - lo], tiles[j])
    attention = jnp.concatenate(tiles, axis=1)
    rows = (residual_ref[...].astype(jnp.float32) + attention).astype(out_ref.dtype)
    out_ref[...] = rows
    for k in range(copies_ref.shape[0]):
        copies_ref[k] = rows


def combine(source_sum, source_stats, residual_rows, copies):
    heads = source_stats.shape[-1] // 2
    source_count, row_count, width = source_sum.shape
    rows = 16 if row_count % 16 == 0 else row_count
    return pl.pallas_call(
        functools.partial(combine_kernel, heads=heads),
        grid=(row_count // rows,),
        in_specs=[
            pl.BlockSpec((source_count, rows, width), lambda i: (0, i, 0)),
            pl.BlockSpec((source_count, rows, 2 * heads), lambda i: (0, i, 0)),
            pl.BlockSpec((rows, width), lambda i: (i, 0)),
        ],
        out_specs=[
            pl.BlockSpec((rows, width), lambda i: (i, 0)),
            pl.BlockSpec((copies, rows, width), lambda i: (0, i, 0)),
        ],
        out_shape=[
            jax.ShapeDtypeStruct(residual_rows.shape, jnp.bfloat16),
            jax.ShapeDtypeStruct((copies,) + residual_rows.shape, jnp.bfloat16),
        ],
    )(source_sum, source_stats, residual_rows)


def normalize(features, norm_gain):
    values = features.astype(jnp.float32)
    mean_square = jnp.mean(values * values, axis=-1, keepdims=True)
    return (values * lax.rsqrt(mean_square + 1e-05) * norm_gain).astype(jnp.bfloat16)


def per_device(
    queries, new_kv, cache_kv, cached_len, residual_in, norm_gain, gate_w, up_w, down_w, owner
):
    slot_count, token_count, width_local = queries.shape
    head_count = width_local // HEAD
    seq_index = lax.axis_index("seq")
    seq_count = lax.axis_size("seq")
    all_queries = lax.all_to_all(
        jnp.broadcast_to(queries[None], (seq_count,) + queries.shape), "seq", 0, 0, tiled=True
    )
    partial_sum, partial_stats = local_attention(all_queries, cache_kv, new_kv, cached_len, seq_index)
    source_sum = lax.all_to_all(partial_sum, "seq", 0, 0, tiled=True)
    source_stats = lax.all_to_all(partial_stats, "seq", 0, 0, tiled=True)
    row_count = slot_count * token_count
    tp_count = lax.axis_size("tp")
    block_rows, row_copies = combine(
        source_sum.reshape(seq_count, row_count, width_local),
        source_stats.reshape(seq_count, row_count, 2 * head_count),
        residual_in.reshape(row_count, width_local),
        tp_count,
    )
    full_rows = (
        lax.all_to_all(
            row_copies, "tp", 0, 0, tiled=True
        )
        .transpose(1, 0, 2)
        .reshape(row_count, tp_count * width_local)
    )
    normed = normalize(full_rows, norm_gain)
    gate_out = jnp.dot(normed, gate_w, preferred_element_type=jnp.float32)
    up_out = jnp.dot(normed, up_w, preferred_element_type=jnp.float32)
    hidden = (jax.nn.silu(gate_out) * up_out).astype(jnp.bfloat16)
    partial_sum = jnp.dot(hidden, down_w, preferred_element_type=jnp.float32)
    pieces = partial_sum.astype(jnp.bfloat16).reshape(row_count, tp_count, width_local).transpose(1, 0, 2)
    unit_share = jnp.sum(
        lax.all_to_all(pieces, "tp", 0, 0, tiled=True).astype(jnp.float32), axis=0
    )
    finished = (block_rows.astype(jnp.float32) + unit_share).astype(jnp.bfloat16)

    owner_ids = owner.reshape(-1)
    owner_count = lax.axis_size(("req", "seq"))
    slot_cap = max(2, 2 * row_count // owner_count)
    matches = (owner_ids[:, None] == jnp.arange(owner_count, dtype=jnp.int32)[None, :]).astype(
        jnp.int32
    )
    ranking = jnp.sum(jnp.cumsum(matches, axis=0) * matches, axis=1) - 1
    outgoing = (
        jnp.zeros((owner_count * slot_cap, width_local), jnp.bfloat16)
        .at[owner_ids * slot_cap + ranking]
        .set(finished)
    )
    incoming = lax.all_to_all(
        outgoing.reshape(owner_count, slot_cap, width_local),
        ("req", "seq"),
        split_axis=0,
        concat_axis=0,
        tiled=True,
    )
    return incoming.reshape(1, owner_count, slot_cap, width_local)


def solution(mesh):
    return jax.shard_map(
        per_device,
        mesh=mesh,
        in_specs=(
            P("req", "seq", "tp"),
            P("req", "seq", None, "tp"),
            P("req", "seq", None, "tp"),
            P("req"),
            P("req", "seq", "tp"),
            P(),
            P(None, "tp"),
            P(None, "tp"),
            P("tp", None),
            P(("req", "seq"), None, None),
        ),
        out_specs=P(("req", "seq"), None, None, "tp"),
        check_vma=False,
    )
```

```python
import functools

import jax
import jax.numpy as jnp
from jax import lax
from jax.experimental import pallas as pl
from jax.experimental.pallas import tpu as pltpu
from jax.sharding import PartitionSpec as P

HEAD = 96

masked_floor = -1e30
LANE = 128
KEY_BLOCK = 256


def attention_kernel(meta_ref, q_ref, kc_ref, vc_ref, kf_ref, vf_ref, sum_ref, stat_ref, *, tq, heads):
    slot = pl.program_id(0)
    q_block = pl.program_id(1)
    seq_index = meta_ref[0]
    length = meta_ref[1 + slot]
    span = kc_ref.shape[0]
    fresh_count = kf_ref.shape[0]
    width = q_ref.shape[-1]
    offset = seq_index * span
    scale = HEAD ** (-0.5)

    q = q_ref[...].reshape(tq, q_ref.shape[-1])
    lane = lax.broadcasted_iota(jnp.int32, (1, width), 1)
    stat_lane = lax.broadcasted_iota(jnp.int32, (1, 2 * heads), 1)
    rows = q_block * tq + lax.broadcasted_iota(jnp.int32, (tq, 1), 0)
    fresh_cols = seq_index * fresh_count + lax.broadcasted_iota(jnp.int32, (1, fresh_count), 1)
    fresh_visible = fresh_cols <= rows
    cached_visible = (offset + lax.broadcasted_iota(jnp.int32, (1, span), 1)) < length
    contract = (((1,), (1,)), ((), ()))

    def run(with_cache, masked=True, keys=span):
        kf = kf_ref[...]
        vf = vf_ref[...]
        if with_cache:
            kc = kc_ref[:keys, :]
            vc = vc_ref[:keys, :]
            visible = cached_visible[:, :keys]
        tiles = [jnp.zeros((tq, LANE), jnp.float32) for _ in range(width // LANE)]
        stats = jnp.zeros((tq, 2 * heads), jnp.float32)
        for h in range(heads):
            lo = h * HEAD // LANE * LANE
            hi = -(-(h + 1) * HEAD // LANE) * LANE
            head_lanes = (lane >= h * HEAD) & (lane < (h + 1) * HEAD)
            qh = jnp.where(head_lanes[:, lo:hi], q[:, lo:hi], jnp.zeros_like(q[:, lo:hi]))
            sf = lax.dot_general(qh, kf[:, lo:hi], contract, preferred_element_type=jnp.float32)
            sf = jnp.where(fresh_visible, sf, masked_floor)
            peak = jnp.max(sf, axis=-1, keepdims=True)
            if with_cache:
                sc = lax.dot_general(qh, kc[:, lo:hi], contract, preferred_element_type=jnp.float32)
                if masked:
                    sc = jnp.where(visible, sc, masked_floor)
                peak = jnp.maximum(peak, jnp.max(sc, axis=-1, keepdims=True))
            pf = jnp.where(fresh_visible, jnp.exp((sf - peak) * scale), 0.0)
            total = jnp.sum(pf, axis=-1, keepdims=True)
            oh = jnp.dot(pf.astype(jnp.bfloat16), vf[:, lo:hi], preferred_element_type=jnp.float32)
            if with_cache:
                pc = jnp.exp((sc - peak) * scale)
                total = total + jnp.sum(pc, axis=-1, keepdims=True)
                oh = oh + jnp.dot(pc.astype(jnp.bfloat16), vc[:, lo:hi], preferred_element_type=jnp.float32)
            for j in range(lo // LANE, hi // LANE):
                part = oh[:, j * LANE - lo:(j + 1) * LANE - lo]
                tiles[j] = jnp.where(head_lanes[:, j * LANE:(j + 1) * LANE], part, tiles[j])
            stats = jnp.where(stat_lane == h, peak * scale, stats)
            stats = jnp.where(stat_lane == heads + h, total, stats)
        weighted = jnp.concatenate(tiles, axis=1)
        sum_ref[...] = weighted.reshape(sum_ref.shape).astype(sum_ref.dtype)
        stat_ref[...] = stats.reshape(stat_ref.shape)

    partial = (offset < length) & (offset + span > length)
    key_blocks = span // KEY_BLOCK
    used_blocks = (length - offset + KEY_BLOCK - 1) // KEY_BLOCK
    for used in range(1, key_blocks + 1):

        @pl.when(partial & (used_blocks == used))
        def _():
            run(True, keys=used * KEY_BLOCK)

    @pl.when(offset + span <= length)
    def _():
        run(True, masked=False)

    @pl.when(offset >= length)
    def _():
        run(False)


def local_attention(all_queries, cache_kv, new_kv, cached_len, seq_index):
    source_count, slot_count, token_count, width = all_queries.shape
    query_count = source_count * token_count
    span = cache_kv.shape[1]
    fresh_count = new_kv.shape[1]
    heads = width // HEAD
    tq = query_count
    cache2 = cache_kv.transpose(0, 2, 1, 3)
    fresh2 = new_kv.transpose(0, 2, 1, 3)
    meta = jnp.concatenate([jnp.reshape(seq_index, (1,)).astype(jnp.int32), cached_len.astype(jnp.int32)])
    kernel = functools.partial(attention_kernel, tq=tq, heads=heads)
    grid_spec = pltpu.PrefetchScalarGridSpec(
        num_scalar_prefetch=1,
        grid=(slot_count, query_count // tq),
        in_specs=[
            pl.BlockSpec((tq // token_count, None, token_count, width), lambda s, b, m: (b, s, 0, 0)),
            pl.BlockSpec((None, None, span, width), lambda s, b, m: (s, 0, 0, 0)),
            pl.BlockSpec((None, None, span, width), lambda s, b, m: (s, 1, 0, 0)),
            pl.BlockSpec((None, None, fresh_count, width), lambda s, b, m: (s, 0, 0, 0)),
            pl.BlockSpec((None, None, fresh_count, width), lambda s, b, m: (s, 1, 0, 0)),
        ],
        out_specs=[
            pl.BlockSpec((tq // token_count, None, token_count, width), lambda s, b, m: (b, s, 0, 0)),
            pl.BlockSpec((tq // token_count, None, token_count, 2 * heads), lambda s, b, m: (b, s, 0, 0)),
        ],
    )
    return pl.pallas_call(
        kernel,
        grid_spec=grid_spec,
        out_shape=[
            jax.ShapeDtypeStruct((source_count, slot_count, token_count, width), jnp.bfloat16),
            jax.ShapeDtypeStruct((source_count, slot_count, token_count, 2 * heads), jnp.float32),
        ],
    )(meta, all_queries, cache2, cache2, fresh2, fresh2)


def combine_kernel(sum_ref, stat_ref, residual_ref, out_ref, copies_ref, *, heads):
    stats = stat_ref[...]
    width = sum_ref.shape[-1]
    lane = lax.broadcasted_iota(jnp.int32, (1, width), 1)
    tiles = [jnp.zeros((sum_ref.shape[1], LANE), jnp.float32) for _ in range(width // LANE)]
    for h in range(heads):
        lo = h * HEAD // LANE * LANE
        hi = -(-(h + 1) * HEAD // LANE) * LANE
        peak = stats[:, :, h:h + 1]
        joint_peak = jnp.max(peak, axis=0)
        scale = jnp.exp(peak - joint_peak[None])
        total = jnp.sum(stats[:, :, heads + h:heads + h + 1] * scale, axis=0)
        head_sum = jnp.sum(sum_ref[:, :, lo:hi].astype(jnp.float32) * scale, axis=0)
        value = head_sum / total
        for j in range(lo // LANE, hi // LANE):
            head_lanes = (lane[:, j * LANE:(j + 1) * LANE] >= h * HEAD) & (
                lane[:, j * LANE:(j + 1) * LANE] < (h + 1) * HEAD
            )
            tiles[j] = jnp.where(head_lanes, value[:, j * LANE - lo:(j + 1) * LANE - lo], tiles[j])
    attention = jnp.concatenate(tiles, axis=1)
    rows = (residual_ref[...].astype(jnp.float32) + attention).astype(out_ref.dtype)
    out_ref[...] = rows
    for k in range(copies_ref.shape[0]):
        copies_ref[k] = rows


def combine(source_sum, source_stats, residual_rows, copies):
    heads = source_stats.shape[-1] // 2
    return pl.pallas_call(
        functools.partial(combine_kernel, heads=heads),
        out_shape=[
            jax.ShapeDtypeStruct(residual_rows.shape, jnp.bfloat16),
            jax.ShapeDtypeStruct((copies,) + residual_rows.shape, jnp.bfloat16),
        ],
    )(source_sum, source_stats, residual_rows)


def copies_kernel(x_ref, out_ref):
    x = x_ref[...]
    for k in range(out_ref.shape[0]):
        out_ref[k] = x


def replicate(x, copies):
    return pl.pallas_call(
        copies_kernel,
        out_shape=jax.ShapeDtypeStruct((copies,) + x.shape, x.dtype),
    )(x)


def normalize(features, norm_gain):
    values = features.astype(jnp.float32)
    mean_square = jnp.mean(values * values, axis=-1, keepdims=True)
    return (values * lax.rsqrt(mean_square + 1e-05) * norm_gain).astype(jnp.bfloat16)


def per_device(
    queries, new_kv, cache_kv, cached_len, residual_in, norm_gain, gate_w, up_w, down_w, owner
):
    slot_count, token_count, width_local = queries.shape
    head_count = width_local // HEAD
    seq_index = lax.axis_index("seq")
    seq_count = lax.axis_size("seq")
    all_queries = lax.all_to_all(replicate(queries, seq_count), "seq", 0, 0, tiled=True)
    partial_sum, partial_stats = local_attention(all_queries, cache_kv, new_kv, cached_len, seq_index)
    source_sum = lax.all_to_all(partial_sum, "seq", 0, 0, tiled=True)
    source_stats = lax.all_to_all(partial_stats, "seq", 0, 0, tiled=True)
    row_count = slot_count * token_count
    tp_count = lax.axis_size("tp")
    block_rows, row_copies = combine(
        source_sum.reshape(seq_count, row_count, width_local),
        source_stats.reshape(seq_count, row_count, 2 * head_count),
        residual_in.reshape(row_count, width_local),
        tp_count,
    )
    full_rows = (
        lax.all_to_all(
            row_copies, "tp", 0, 0, tiled=True
        )
        .transpose(1, 0, 2)
        .reshape(row_count, tp_count * width_local)
    )
    normed = normalize(full_rows, norm_gain)
    gate_out = jnp.dot(normed, gate_w, preferred_element_type=jnp.float32)
    up_out = jnp.dot(normed, up_w, preferred_element_type=jnp.float32)
    hidden = (jax.nn.silu(gate_out) * up_out).astype(jnp.bfloat16)
    partial_sum = jnp.dot(hidden, down_w, preferred_element_type=jnp.float32)
    pieces = partial_sum.astype(jnp.bfloat16).reshape(row_count, tp_count, width_local).transpose(1, 0, 2)
    unit_share = jnp.sum(
        lax.all_to_all(pieces, "tp", 0, 0, tiled=True).astype(jnp.float32), axis=0
    )
    finished = (block_rows.astype(jnp.float32) + unit_share).astype(jnp.bfloat16)

    owner_ids = owner.reshape(-1)
    owner_count = lax.axis_size(("req", "seq"))
    slot_cap = max(2, 2 * row_count // owner_count)
    matches = (owner_ids[:, None] == jnp.arange(owner_count, dtype=jnp.int32)[None, :]).astype(
        jnp.int32
    )
    ranking = jnp.sum(jnp.cumsum(matches, axis=0) * matches, axis=1) - 1
    outgoing = (
        jnp.zeros((owner_count * slot_cap, width_local), jnp.bfloat16)
        .at[owner_ids * slot_cap + ranking]
        .set(finished)
    )
    incoming = lax.all_to_all(
        outgoing.reshape(owner_count, slot_cap, width_local),
        ("req", "seq"),
        split_axis=0,
        concat_axis=0,
        tiled=True,
    )
    return incoming.reshape(1, owner_count, slot_cap, width_local)


def solution(mesh):
    return jax.shard_map(
        per_device,
        mesh=mesh,
        in_specs=(
            P("req", "seq", "tp"),
            P("req", "seq", None, "tp"),
            P("req", "seq", None, "tp"),
            P("req"),
            P("req", "seq", "tp"),
            P(),
            P(None, "tp"),
            P(None, "tp"),
            P("tp", None),
            P(("req", "seq"), None, None),
        ),
        out_specs=P(("req", "seq"), None, None, "tp"),
        check_vma=False,
    )
```

```python
import functools

import jax
import jax.numpy as jnp
from jax import lax
from jax.experimental import pallas as pl
from jax.experimental.pallas import tpu as pltpu
from jax.sharding import PartitionSpec as P

HEAD = 96

masked_floor = -1e30
LANE = 128
KEY_BLOCK = 256


def attention_kernel(meta_ref, q_ref, kc_ref, vc_ref, kf_ref, vf_ref, sum_ref, stat_ref, *, tq, heads):
    slot = pl.program_id(0)
    q_block = pl.program_id(1)
    seq_index = meta_ref[0]
    length = meta_ref[1 + slot]
    span = kc_ref.shape[0]
    fresh_count = kf_ref.shape[0]
    width = q_ref.shape[-1]
    offset = seq_index * span
    scale = HEAD ** (-0.5)

    q = q_ref[...].reshape(tq, q_ref.shape[-1])
    lane = lax.broadcasted_iota(jnp.int32, (1, width), 1)
    stat_lane = lax.broadcasted_iota(jnp.int32, (1, 2 * heads), 1)
    rows = q_block * tq + lax.broadcasted_iota(jnp.int32, (tq, 1), 0)
    fresh_cols = seq_index * fresh_count + lax.broadcasted_iota(jnp.int32, (1, fresh_count), 1)
    fresh_visible = fresh_cols <= rows
    cached_visible = (offset + lax.broadcasted_iota(jnp.int32, (1, span), 1)) < length
    contract = (((1,), (1,)), ((), ()))

    def run(with_cache, masked=True, keys=span):
        kf = kf_ref[...]
        vf = vf_ref[...]
        if with_cache:
            kc = kc_ref[:keys, :]
            vc = vc_ref[:keys, :]
            visible = cached_visible[:, :keys]
        tiles = [jnp.zeros((tq, LANE), jnp.float32) for _ in range(width // LANE)]
        stats = jnp.zeros((tq, 2 * heads), jnp.float32)
        for h in range(heads):
            lo = h * HEAD // LANE * LANE
            hi = -(-(h + 1) * HEAD // LANE) * LANE
            head_lanes = (lane >= h * HEAD) & (lane < (h + 1) * HEAD)
            qh = jnp.where(head_lanes[:, lo:hi], q[:, lo:hi], jnp.zeros_like(q[:, lo:hi]))
            sf = lax.dot_general(qh, kf[:, lo:hi], contract, preferred_element_type=jnp.float32)
            sf = jnp.where(fresh_visible, sf, masked_floor)
            peak = jnp.max(sf, axis=-1, keepdims=True)
            if with_cache:
                sc = lax.dot_general(qh, kc[:, lo:hi], contract, preferred_element_type=jnp.float32)
                if masked:
                    sc = jnp.where(visible, sc, masked_floor)
                peak = jnp.maximum(peak, jnp.max(sc, axis=-1, keepdims=True))
            pf = jnp.where(fresh_visible, jnp.exp((sf - peak) * scale), 0.0)
            total = jnp.sum(pf, axis=-1, keepdims=True)
            oh = jnp.dot(pf.astype(jnp.bfloat16), vf[:, lo:hi], preferred_element_type=jnp.float32)
            if with_cache:
                pc = jnp.exp((sc - peak) * scale)
                total = total + jnp.sum(pc, axis=-1, keepdims=True)
                oh = oh + jnp.dot(pc.astype(jnp.bfloat16), vc[:, lo:hi], preferred_element_type=jnp.float32)
            for j in range(lo // LANE, hi // LANE):
                part = oh[:, j * LANE - lo:(j + 1) * LANE - lo]
                tiles[j] = jnp.where(head_lanes[:, j * LANE:(j + 1) * LANE], part, tiles[j])
            stats = jnp.where(stat_lane == h, peak * scale, stats)
            stats = jnp.where(stat_lane == heads + h, total, stats)
        weighted = jnp.concatenate(tiles, axis=1)
        sum_ref[...] = weighted.reshape(sum_ref.shape).astype(sum_ref.dtype)
        stat_ref[...] = stats.reshape(stat_ref.shape)

    partial = (offset < length) & (offset + span > length)
    key_blocks = span // KEY_BLOCK
    used_blocks = (length - offset + KEY_BLOCK - 1) // KEY_BLOCK
    for used in range(1, key_blocks + 1):

        @pl.when(partial & (used_blocks == used))
        def _():
            run(True, keys=used * KEY_BLOCK)

    @pl.when(offset + span <= length)
    def _():
        run(True, masked=False)

    @pl.when(offset >= length)
    def _():
        run(False)


def local_attention(all_queries, cache_kv, new_kv, cached_len, seq_index):
    source_count, slot_count, token_count, width = all_queries.shape
    query_count = source_count * token_count
    span = cache_kv.shape[1]
    fresh_count = new_kv.shape[1]
    heads = width // HEAD
    tq = query_count
    cache2 = cache_kv.transpose(0, 2, 1, 3)
    fresh2 = new_kv.transpose(0, 2, 1, 3)
    meta = jnp.concatenate([jnp.reshape(seq_index, (1,)).astype(jnp.int32), cached_len.astype(jnp.int32)])
    kernel = functools.partial(attention_kernel, tq=tq, heads=heads)
    grid_spec = pltpu.PrefetchScalarGridSpec(
        num_scalar_prefetch=1,
        grid=(slot_count, query_count // tq),
        in_specs=[
            pl.BlockSpec((tq // token_count, None, token_count, width), lambda s, b, m: (b, s, 0, 0)),
            pl.BlockSpec((None, None, span, width), lambda s, b, m: (s, 0, 0, 0)),
            pl.BlockSpec((None, None, span, width), lambda s, b, m: (s, 1, 0, 0)),
            pl.BlockSpec((None, None, fresh_count, width), lambda s, b, m: (s, 0, 0, 0)),
            pl.BlockSpec((None, None, fresh_count, width), lambda s, b, m: (s, 1, 0, 0)),
        ],
        out_specs=[
            pl.BlockSpec((tq // token_count, None, token_count, width), lambda s, b, m: (b, s, 0, 0)),
            pl.BlockSpec((tq // token_count, None, token_count, 2 * heads), lambda s, b, m: (b, s, 0, 0)),
        ],
    )
    return pl.pallas_call(
        kernel,
        grid_spec=grid_spec,
        out_shape=[
            jax.ShapeDtypeStruct((source_count, slot_count, token_count, width), jnp.bfloat16),
            jax.ShapeDtypeStruct((source_count, slot_count, token_count, 2 * heads), jnp.float32),
        ],
    )(meta, all_queries, cache2, cache2, fresh2, fresh2)


def combine_kernel(sum_ref, stat_ref, residual_ref, out_ref, copies_ref, *, heads):
    stats = stat_ref[...]
    width = sum_ref.shape[-1]
    lane = lax.broadcasted_iota(jnp.int32, (1, width), 1)
    tiles = [jnp.zeros((sum_ref.shape[1], LANE), jnp.float32) for _ in range(width // LANE)]
    peaks = stats[:, :, :heads]
    scales = jnp.exp(peaks - jnp.max(peaks, axis=0)[None])
    totals = jnp.sum(stats[:, :, heads:] * scales, axis=0)
    for h in range(heads):
        lo = h * HEAD // LANE * LANE
        hi = -(-(h + 1) * HEAD // LANE) * LANE
        scale = scales[:, :, h:h + 1]
        total = totals[:, h:h + 1]
        head_sum = jnp.sum(sum_ref[:, :, lo:hi].astype(jnp.float32) * scale, axis=0)
        value = head_sum / total
        for j in range(lo // LANE, hi // LANE):
            head_lanes = (lane[:, j * LANE:(j + 1) * LANE] >= h * HEAD) & (
                lane[:, j * LANE:(j + 1) * LANE] < (h + 1) * HEAD
            )
            tiles[j] = jnp.where(head_lanes, value[:, j * LANE - lo:(j + 1) * LANE - lo], tiles[j])
    attention = jnp.concatenate(tiles, axis=1)
    rows = (residual_ref[...].astype(jnp.float32) + attention).astype(out_ref.dtype)
    out_ref[...] = rows
    for k in range(copies_ref.shape[0]):
        copies_ref[k] = rows


def combine(source_sum, source_stats, residual_rows, copies):
    heads = source_stats.shape[-1] // 2
    return pl.pallas_call(
        functools.partial(combine_kernel, heads=heads),
        out_shape=[
            jax.ShapeDtypeStruct(residual_rows.shape, jnp.bfloat16),
            jax.ShapeDtypeStruct((copies,) + residual_rows.shape, jnp.bfloat16),
        ],
    )(source_sum, source_stats, residual_rows)


def normalize(features, norm_gain):
    values = features.astype(jnp.float32)
    mean_square = jnp.mean(values * values, axis=-1, keepdims=True)
    return (values * lax.rsqrt(mean_square + 1e-05) * norm_gain).astype(jnp.bfloat16)


def per_device(
    queries, new_kv, cache_kv, cached_len, residual_in, norm_gain, gate_w, up_w, down_w, owner
):
    slot_count, token_count, width_local = queries.shape
    head_count = width_local // HEAD
    seq_index = lax.axis_index("seq")
    seq_count = lax.axis_size("seq")
    all_queries = lax.all_to_all(
        jnp.broadcast_to(queries[None], (seq_count,) + queries.shape), "seq", 0, 0, tiled=True
    )
    partial_sum, partial_stats = local_attention(all_queries, cache_kv, new_kv, cached_len, seq_index)
    source_sum = lax.all_to_all(partial_sum, "seq", 0, 0, tiled=True)
    source_stats = lax.all_to_all(partial_stats, "seq", 0, 0, tiled=True)
    row_count = slot_count * token_count
    tp_count = lax.axis_size("tp")
    block_rows, row_copies = combine(
        source_sum.reshape(seq_count, row_count, width_local),
        source_stats.reshape(seq_count, row_count, 2 * head_count),
        residual_in.reshape(row_count, width_local),
        tp_count,
    )
    full_rows = (
        lax.all_to_all(
            row_copies, "tp", 0, 0, tiled=True
        )
        .transpose(1, 0, 2)
        .reshape(row_count, tp_count * width_local)
    )
    normed = normalize(full_rows, norm_gain)
    gate_out = jnp.dot(normed, gate_w, preferred_element_type=jnp.float32)
    up_out = jnp.dot(normed, up_w, preferred_element_type=jnp.float32)
    hidden = (jax.nn.silu(gate_out) * up_out).astype(jnp.bfloat16)
    partial_sum = jnp.dot(hidden, down_w, preferred_element_type=jnp.float32)
    pieces = partial_sum.astype(jnp.bfloat16).reshape(row_count, tp_count, width_local).transpose(1, 0, 2)
    unit_share = jnp.sum(
        lax.all_to_all(pieces, "tp", 0, 0, tiled=True).astype(jnp.float32), axis=0
    )
    finished = (block_rows.astype(jnp.float32) + unit_share).astype(jnp.bfloat16)

    owner_ids = owner.reshape(-1)
    owner_count = lax.axis_size(("req", "seq"))
    slot_cap = max(2, 2 * row_count // owner_count)
    matches = (owner_ids[:, None] == jnp.arange(owner_count, dtype=jnp.int32)[None, :]).astype(
        jnp.int32
    )
    ranking = jnp.sum(jnp.cumsum(matches, axis=0) * matches, axis=1) - 1
    outgoing = (
        jnp.zeros((owner_count * slot_cap, width_local), jnp.bfloat16)
        .at[owner_ids * slot_cap + ranking]
        .set(finished)
    )
    incoming = lax.all_to_all(
        outgoing.reshape(owner_count, slot_cap, width_local),
        ("req", "seq"),
        split_axis=0,
        concat_axis=0,
        tiled=True,
    )
    return incoming.reshape(1, owner_count, slot_cap, width_local)


def solution(mesh):
    return jax.shard_map(
        per_device,
        mesh=mesh,
        in_specs=(
            P("req", "seq", "tp"),
            P("req", "seq", None, "tp"),
            P("req", "seq", None, "tp"),
            P("req"),
            P("req", "seq", "tp"),
            P(),
            P(None, "tp"),
            P(None, "tp"),
            P("tp", None),
            P(("req", "seq"), None, None),
        ),
        out_specs=P(("req", "seq"), None, None, "tp"),
        check_vma=False,
    )
```
